256 devices in a mesh: dp: 32 (over x, z_lo, core), fsdp: 8 (over y, z_hi).
Axes of the slice: x: 4, y: 4, z: 8 (z_hi: 2, z_lo: 4; z = z_hi * 4 + z_lo), core: 2. Of those that a mesh axis runs over, the one named last changes fastest.
Arguments:
- stream_rows: bfloat16 [16384, 4096], P(('dp', 'fsdp')), may hold values from -6 to 6
- ln_gain: float32 [4096], replicated, may hold values from 0.1 to 1.9
- ln_bias: float32 [4096], replicated, may hold values from -2 to 2
- w_q: bfloat16 [4096, 2048], P(None, 'fsdp')
- w_k: bfloat16 [4096, 2048], P(None, 'fsdp')
- w_v: bfloat16 [4096, 2048], P(None, 'fsdp'), may hold values from -0.09375 to 0.09375
- w_o: bfloat16 [2048, 4096], P('fsdp'), may hold values from -0.1875 to 0.1875
- scale_ls: float32 [4096], P('fsdp'), may hold values from 0.5 to 2
- sides: int32 [32, 1], P('dp'), may hold values from 10 to 18, as said below
- offsets: int32 [32, 1], P('dp'), may hold values from 0 to 0, as said below
- owners: int32 [32, 1], replicated, may hold values from 0 to 31, as said below
Outputs:
- delivered: bfloat16 [32, 1, 81, 4, 4096], P('dp', None, None, None, 'fsdp')
The draws below stay inside these ranges and needn't reach their ends.
Inputs may be any that keep to these rules, and one draw needn't show every extreme that they name: `sides`: every side is even, and some image has side 18 in every draw. `offsets`: within a group the images lie back to back in index order from row 0, each taking 5 + side * side rows; the rows after the last image are padding. owners[g, j] = (g + c_j) mod 32, with offsets c_j that differ between image indices j; so the images of one group have different owners and every owner receives exactly one image of each index j.
All inputs are finite; a program needn't handle non-finite values.
Results may differ from the reference program's by a relative error of at most 0.012.
Values may be sent and summed in bfloat16 or wider, within the bound.
No kernel may reach another device: no remote copies, remote signals or barrier semaphores. Data moves between devices by JAX's collectives and lax.ppermute only.
A program may use at most 128 MiB of HBM per device.

```python
import math
import jax
import jax.numpy as jnp
from jax import lax

D = 4096
HEADS = 16
HEAD = 128
EXTRA = 5
MINSIDE = 10
MAXSIDE = 18
GT = 512
IMGS = 1
CAP = 81
GROUPS = 32
ROWS = 16384
N_FSDP = 8


def grid_sides(key):
    steps_drawn = jax.random.randint(jax.random.fold_in(key, 11), (GROUPS, IMGS), 0, 5)
    side_grid = MINSIDE + 2 * steps_drawn
    chosen = jax.random.randint(jax.random.fold_in(key, 12), (), 0, GROUPS * IMGS)
    flat = side_grid.reshape(-1).at[chosen].set(MAXSIDE)
    return flat.reshape(GROUPS, IMGS).astype(jnp.int32)


def draw_sides(key, part):
    return grid_sides(key)


def draw_offsets(key, part):
    side_grid = grid_sides(key)
    lengths = EXTRA + side_grid * side_grid
    return (jnp.cumsum(lengths, axis=1) - lengths).astype(jnp.int32)


def draw_owners(key, part):
    order = jax.random.permutation(jax.random.fold_in(key, 21), GROUPS).astype(jnp.int32)
    offsets_drawn = order[:IMGS]
    group_ids = jnp.arange(GROUPS, dtype=jnp.int32)
    return ((group_ids[:, None] + offsets_drawn[None, :]) % GROUPS).astype(jnp.int32)


def projection_pair(key):
    base = jax.random.normal(jax.random.fold_in(key, 31), (D, HEADS * HEAD), jnp.float32) / math.sqrt(D)
    other = jax.random.normal(jax.random.fold_in(key, 32), (D, HEADS * HEAD), jnp.float32) / math.sqrt(D)
    paired = other
    return (base, paired)


def draw_w_q(key, part):
    return projection_pair(key)[0].astype(jnp.bfloat16)


def draw_w_k(key, part):
    return projection_pair(key)[1].astype(jnp.bfloat16)


def with_spikes(drawn, key, source, target, parts, factor):
    def block_of(axis_at):
        return (jnp.arange(drawn.shape[axis_at]) // (drawn.shape[axis_at] // parts)).reshape((-1,) + (1,) * (drawn.ndim - 1 - axis_at))

    one_side = jax.random.permutation(key, parts)[block_of(target)]
    far = (block_of(target) + parts // 2) % parts
    return jnp.where((block_of(source) == one_side) | (block_of(source) == far), factor * drawn, drawn)


def level_of(own_key, shape, split, least, high):
    def one(dim, shards_of):
        draws = jax.random.uniform(jax.random.fold_in(jax.random.fold_in(own_key, 6), dim), (shards_of,), jnp.float32, least / len(split), high / len(split))
        return jnp.repeat(jnp.exp(draws), shape[dim] // shards_of).reshape((-1,) + (1,) * (len(shape) - dim - 1))

    level = one(*split[0])
    for cut in split[1:]:
        level = level * one(*cut)
    return level


def normal_values(stream_key, shape, width, most, split=(), kind=jnp.bfloat16):
    array = width * jax.random.normal(stream_key, shape, jnp.float32)
    if split:
        array = array * level_of(stream_key, shape, split, -0.22, 0.18)
    return jnp.clip(array, -most, most).astype(kind)


def noise_with(rng, extent, scale, limit, split, heavy, kind=jnp.bfloat16):
    result = scale * jax.random.normal(rng, extent, jnp.float32)
    if split:
        result = result * level_of(rng, extent, split, -0.22, 0.18)
    return jnp.clip(with_spikes(result, jax.random.fold_in(rng, 3), *heavy), -limit, limit).astype(kind)


def setup_inputs(seed: int = 0) -> dict:
    keys = jax.random.split(jax.random.key(seed), 12)
    return {
        "stream_rows": normal_values(keys[0], (ROWS, D), 1.0, 6.0, ((0, 256),)),
        "ln_gain": jnp.clip(1.0 + 0.18 * jax.random.normal(keys[1], (D,), jnp.float32), 0.1, 1.9),
        "ln_bias": normal_values(keys[2], (D,), 0.3, 2.0, (), jnp.float32),
        "w_q": draw_w_q(jax.random.fold_in(keys[11], 71), 0),
        "w_k": draw_w_k(jax.random.fold_in(keys[11], 71), 0),
        "w_v": normal_values(keys[5], (D, HEADS * HEAD), D ** -0.5, 0.09375, ((1, 8),)),
        "w_o": noise_with(keys[6], (HEADS * HEAD, D), (HEADS * HEAD) ** -0.5, 0.1875, ((0, 8),), (0, 1, 8, 2.0)),
        "scale_ls": jnp.clip(jnp.exp(math.log(2.0) - 1.3862944 * jax.random.uniform(keys[7], (D,), jnp.float32) ** level_of(keys[7], (D,), ((0, 8),), -0.2, 0.2)), 0.5, 2.0),
        "sides": draw_sides(jax.random.fold_in(keys[11], 71), 0),
        "offsets": draw_offsets(jax.random.fold_in(keys[11], 71), 0),
        "owners": draw_owners(jax.random.fold_in(keys[11], 71), 0),
    }


norm_eps = 1e-06

def layer_norm(raw_rows, ln_gain, ln_bias):
    values = raw_rows.astype(jnp.float32)
    centre = lax.optimization_barrier(jnp.mean(values, axis=-1, keepdims=True))
    spread = lax.optimization_barrier(jnp.mean(jnp.square(values - centre), axis=-1, keepdims=True))
    return ((values - centre) * lax.rsqrt(spread + norm_eps) * ln_gain + ln_bias).astype(jnp.bfloat16)

def row_layout(side_row, offset_row, count):
    row_ids = jnp.arange(count, dtype=jnp.int32)
    lengths = EXTRA + side_row * side_row
    inside = ((row_ids[:, None] >= offset_row[None, :]) & (row_ids[:, None] < (offset_row + lengths)[None, :])).astype(jnp.int32)
    covered = lax.optimization_barrier(jnp.sum(inside, axis=1))
    image_ids = jnp.arange(side_row.shape[0], dtype=jnp.int32)
    segment = lax.optimization_barrier(jnp.sum(inside * image_ids[None, :], axis=1)) + (1 - covered) * side_row.shape[0]
    first_row = lax.optimization_barrier(jnp.sum(inside * offset_row[None, :], axis=1))
    side_len = lax.optimization_barrier(jnp.sum(inside * side_row[None, :], axis=1)) + (1 - covered)
    patch_id = row_ids - first_row - EXTRA
    is_patch = (covered == 1) & (patch_id >= 0)
    clipped = jnp.maximum(patch_id, 0)
    across = clipped // side_len
    along = clipped % side_len
    side_float = side_len.astype(jnp.float32)
    coord_one = jnp.where(is_patch, (2 * across + 1).astype(jnp.float32) / side_float - 1.0, jnp.zeros_like(side_float))
    coord_two = jnp.where(is_patch, (2 * along + 1).astype(jnp.float32) / side_float - 1.0, jnp.zeros_like(side_float))
    return (segment, coord_one, coord_two)

def rotary_tables(coord_one, coord_two, head_size):
    dims = jnp.arange(head_size, dtype=jnp.int32)
    first_half = dims < head_size // 2
    freq_index = (dims % (head_size // 4)).astype(jnp.float32)
    rates = 3.0 * jnp.power(jnp.ones_like(freq_index) * 1.2, freq_index)
    coords = jnp.where(first_half[None, :], coord_one[:, None], coord_two[:, None])
    angles = coords * rates[None, :]
    return (jnp.cos(angles), jnp.sin(angles))

def rotate(tensor, cosine, sine_tab):
    row_count, head_count, head_size = tensor.shape
    quarters = tensor.reshape(row_count, head_count, 2, 2, head_size // 4)
    turned = jnp.stack([-quarters[:, :, :, 1], quarters[:, :, :, 0]], axis=3).reshape(tensor.shape)
    return tensor * cosine[:, None, :] + turned * sine_tab[:, None, :]

def softmax_rounded(scores):
    top = lax.optimization_barrier(jnp.max(scores, axis=-1, keepdims=True))
    expo = jnp.exp(scores - top)
    return (expo / lax.optimization_barrier(jnp.sum(expo, axis=-1, keepdims=True))).astype(jnp.bfloat16)

def merge_image(rows_all, side_len, offset):
    slot = jnp.arange(CAP, dtype=jnp.int32)
    half_side = side_len // 2
    across = slot // half_side
    along = slot % half_side
    valid = slot < half_side * half_side
    corner = jnp.arange(4, dtype=jnp.int32)
    source_rows = offset + EXTRA + (2 * across[:, None] + corner[None, :] // 2) * side_len + 2 * along[:, None] + corner[None, :] % 2
    source_rows = jnp.where(valid[:, None], source_rows, jnp.zeros_like(source_rows))
    picked = jnp.take(rows_all, source_rows, axis=0)
    return jnp.where(valid[:, None, None], picked, jnp.zeros_like(picked))

def reference(stream_rows, ln_gain, ln_bias, w_q, w_k, w_v, w_o, scale_ls, sides, offsets, owners):
    group_rows = stream_rows.reshape(GROUPS, GT, D)
    head_cols = HEADS * HEAD
    share = head_cols // N_FSDP

    def encode(entry):
        rows_in, side_row, offset_row = entry
        normed = layer_norm(rows_in, ln_gain, ln_bias)
        segment, coord_one, coord_two = row_layout(side_row, offset_row, GT)
        cosine, sine_tab = rotary_tables(coord_one, coord_two, HEAD)
        queries = rotate(jnp.dot(normed, w_q, preferred_element_type=jnp.float32).reshape(GT, HEADS, HEAD), cosine, sine_tab).astype(jnp.bfloat16)
        key_rows = rotate(jnp.dot(normed, w_k, preferred_element_type=jnp.float32).reshape(GT, HEADS, HEAD), cosine, sine_tab).astype(jnp.bfloat16)
        value_rows = jnp.dot(normed, w_v, preferred_element_type=jnp.float32).astype(jnp.bfloat16).reshape(GT, HEADS, HEAD)
        allowed = segment[:, None] == segment[None, :]

        def one_head(head_id):
            query_head = lax.dynamic_index_in_dim(queries, head_id, 1, keepdims=False)
            key_head = lax.dynamic_index_in_dim(key_rows, head_id, 1, keepdims=False)
            value_head = lax.dynamic_index_in_dim(value_rows, head_id, 1, keepdims=False)
            scores = jnp.dot(query_head, key_head.T, preferred_element_type=jnp.float32) / math.sqrt(HEAD)
            scores = jnp.where(allowed, scores, jnp.full_like(scores, -1e+30))
            weights = softmax_rounded(scores)
            return jnp.dot(weights, value_head, preferred_element_type=jnp.float32).astype(jnp.bfloat16)
        mixed = lax.map(one_head, jnp.arange(HEADS, dtype=jnp.int32))
        attended = jnp.transpose(mixed, (1, 0, 2)).reshape(GT, head_cols)
        branch = jnp.zeros((GT, D), jnp.float32)
        for group in range(N_FSDP):
            part_sum = jnp.dot(attended[:, group * share:(group + 1) * share], w_o[group * share:(group + 1) * share], preferred_element_type=jnp.float32).astype(jnp.bfloat16)
            branch = branch + lax.optimization_barrier(part_sum).astype(jnp.float32)
        updated = (rows_in.astype(jnp.float32) + scale_ls * branch).astype(jnp.bfloat16)
        return jnp.stack([merge_image(updated, side_row[image], offset_row[image]) for image in range(IMGS)])
    merged = lax.map(encode, (group_rows, sides, offsets))
    slot_ids = jnp.broadcast_to(jnp.arange(IMGS, dtype=jnp.int32)[None, :], (GROUPS, IMGS))
    return jnp.zeros_like(merged).at[owners, slot_ids].set(merged)
```

```python
import math

import jax
import jax.numpy as jnp
import numpy as np
from jax import lax
from jax.sharding import Mesh
from jax.sharding import PartitionSpec as P

HEAD = 128
EXTRA = 5
CAP = 81
LIVE_ROWS = 336

norm_eps = 1e-06

DP_AXES = ("x", "zl", "c")
FSDP_AXES = ("y", "zh")


def layer_norm(raw_rows, ln_gain, ln_bias):
    values = raw_rows.astype(jnp.float32)
    centre = jnp.mean(values, axis=-1, keepdims=True)
    spread = jnp.mean(jnp.square(values - centre), axis=-1, keepdims=True)
    return ((values - centre) * lax.rsqrt(spread + norm_eps) * ln_gain + ln_bias).astype(
        jnp.bfloat16
    )


def row_layout(side_row, offset_row, count):
    row_ids = jnp.arange(count, dtype=jnp.int32)
    lengths = EXTRA + side_row * side_row
    inside = (
        (row_ids[:, None] >= offset_row[None, :])
        & (row_ids[:, None] < (offset_row + lengths)[None, :])
    ).astype(jnp.int32)
    covered = jnp.sum(inside, axis=1)
    image_ids = jnp.arange(side_row.shape[0], dtype=jnp.int32)
    segment = jnp.sum(inside * image_ids[None, :], axis=1) + (1 - covered) * side_row.shape[0]
    first_row = jnp.sum(inside * offset_row[None, :], axis=1)
    side_len = jnp.sum(inside * side_row[None, :], axis=1) + (1 - covered)
    patch_id = row_ids - first_row - EXTRA
    is_patch = (covered == 1) & (patch_id >= 0)
    clipped = jnp.maximum(patch_id, 0)
    across = clipped // side_len
    along = clipped % side_len
    side_float = side_len.astype(jnp.float32)
    coord_one = jnp.where(
        is_patch,
        (2 * across + 1).astype(jnp.float32) / side_float - 1.0,
        jnp.zeros_like(side_float),
    )
    coord_two = jnp.where(
        is_patch, (2 * along + 1).astype(jnp.float32) / side_float - 1.0, jnp.zeros_like(side_float)
    )
    return (segment, coord_one, coord_two)


def rotary_tables(coord_one, coord_two, head_size):
    dims = jnp.arange(head_size, dtype=jnp.int32)
    first_half = dims < head_size // 2
    freq_index = (dims % (head_size // 4)).astype(jnp.float32)
    rates = 3.0 * jnp.power(jnp.ones_like(freq_index) * 1.2, freq_index)
    coords = jnp.where(first_half[None, :], coord_one[:, None], coord_two[:, None])
    angles = coords * rates[None, :]
    return (jnp.cos(angles), jnp.sin(angles))


def rotate(tensor, cosine, sine_tab):
    row_count, head_count, head_size = tensor.shape
    quarters = tensor.reshape(row_count, head_count, 2, 2, head_size // 4)
    turned = jnp.stack([-quarters[:, :, :, 1], quarters[:, :, :, 0]], axis=3).reshape(tensor.shape)
    return tensor * cosine[:, None, :] + turned * sine_tab[:, None, :]


def softmax_rounded(scores):
    top = jnp.max(scores, axis=-1, keepdims=True)
    expo = jnp.exp(scores - top)
    return (expo / jnp.sum(expo, axis=-1, keepdims=True)).astype(jnp.bfloat16)


def merge_rows(side_len, offset):
    slot = jnp.arange(CAP, dtype=jnp.int32)
    half_side = side_len // 2
    across = slot // half_side
    along = slot % half_side
    valid = slot < half_side * half_side
    corner = jnp.arange(4, dtype=jnp.int32)
    source_rows = (
        offset
        + EXTRA
        + (2 * across[:, None] + corner[None, :] // 2) * side_len
        + 2 * along[:, None]
        + corner[None, :] % 2
    )
    source_rows = jnp.where(valid[:, None], source_rows, jnp.zeros_like(source_rows))
    return source_rows.reshape(CAP * 4), valid


def attention(queries, key_rows, value_rows, segment):
    scores = jnp.einsum(
        "qhd,khd->hqk", queries, key_rows, preferred_element_type=jnp.float32
    ) / math.sqrt(HEAD)
    allowed = segment[None, :, None] == segment[None, None, :]
    scores = jnp.where(allowed, scores, jnp.full_like(scores, -1e30))
    weights = softmax_rounded(scores)
    return jnp.einsum(
        "hqk,khd->qhd", weights, value_rows, preferred_element_type=jnp.float32
    ).astype(jnp.bfloat16)


def shift_dp(block, distance):
    count = 1
    for name in DP_AXES:
        count *= lax.axis_size(name)

    def branch(by):
        if by == 0:
            return lambda v: v
        pairs = [(i, (i + by) % count) for i in range(count)]
        return lambda v: lax.ppermute(v, DP_AXES, pairs)

    return lax.switch(distance, [branch(by) for by in range(count)], block)


def body(stream_rows, ln_gain, ln_bias, w_q, w_k, w_v, w_o, scale_ls, sides, offsets, owners):
    head_cols = w_q.shape[1]
    local_heads = head_cols // HEAD
    side_row = sides[0]
    offset_row = offsets[0]
    feat_cols = scale_ls.shape[0]

    pair_rows = lax.all_gather(stream_rows, "zh", axis=0, tiled=True)
    group_rows = lax.all_gather(pair_rows, "y", axis=0, tiled=True)
    live_rows = group_rows[:LIVE_ROWS]
    normed = layer_norm(live_rows, ln_gain, ln_bias)

    projected = jnp.concatenate(
        [
            jnp.dot(normed, w_q, preferred_element_type=jnp.float32),
            jnp.dot(normed, w_k, preferred_element_type=jnp.float32),
            jnp.dot(normed, w_v, preferred_element_type=jnp.float32),
        ],
        axis=1,
    )
    segment, coord_one, coord_two = row_layout(side_row, offset_row, LIVE_ROWS)
    cosine, sine_tab = rotary_tables(coord_one, coord_two, HEAD)
    queries = rotate(
        projected[:, :head_cols].reshape(LIVE_ROWS, local_heads, HEAD), cosine, sine_tab
    ).astype(jnp.bfloat16)
    key_rows = rotate(
        projected[:, head_cols : 2 * head_cols].reshape(LIVE_ROWS, local_heads, HEAD),
        cosine,
        sine_tab,
    ).astype(jnp.bfloat16)
    value_rows = (
        projected[:, 2 * head_cols :].astype(jnp.bfloat16).reshape(LIVE_ROWS, local_heads, HEAD)
    )
    attended = attention(queries, key_rows, value_rows, segment).reshape(LIVE_ROWS, head_cols)

    source_rows, valid = merge_rows(side_row[0], offset_row[0])
    merged_attended = jnp.take(attended, source_rows, axis=0)
    partial_sum = jnp.dot(merged_attended, w_o, preferred_element_type=jnp.float32).astype(
        jnp.bfloat16
    )
    quarter = lax.psum_scatter(partial_sum, "y", scatter_dimension=1, tiled=True)
    branch = lax.psum_scatter(quarter, "zh", scatter_dimension=1, tiled=True).astype(jnp.float32)

    feat_index = lax.axis_index("y") * lax.axis_size("zh") + lax.axis_index("zh")
    residual = lax.dynamic_slice_in_dim(
        jnp.take(live_rows, source_rows, axis=0), feat_index * feat_cols, feat_cols, axis=1
    )
    updated = (residual.astype(jnp.float32) + scale_ls * branch).astype(jnp.bfloat16)
    merged = jnp.where(
        jnp.repeat(valid, 4)[:, None], updated, jnp.zeros_like(updated)
    ).reshape(1, CAP, 4, feat_cols)

    group_count = 1
    for name in DP_AXES:
        group_count *= lax.axis_size(name)
    distance = owners[0, 0] % group_count
    delivered = shift_dp(merged, distance)
    return delivered[None]


def solution(mesh):
    dp_size, fsdp_size = mesh.devices.shape
    split_mesh = Mesh(
        np.asarray(mesh.devices).reshape(4, dp_size // 8, 2, fsdp_size // 2, 2),
        DP_AXES + FSDP_AXES,
    )
    rows = DP_AXES + FSDP_AXES
    return jax.shard_map(
        body,
        mesh=split_mesh,
        in_specs=(
            P(rows, None),
            P(),
            P(),
            P(None, FSDP_AXES),
            P(None, FSDP_AXES),
            P(None, FSDP_AXES),
            P(FSDP_AXES, None),
            P(FSDP_AXES),
            P(DP_AXES, None),
            P(DP_AXES, None),
            P(),
        ),
        out_specs=P(DP_AXES, None, None, None, FSDP_AXES),
        check_vma=False,
    )
```

```python
import math

import jax
import jax.numpy as jnp
import numpy as np
from jax import lax
from jax.sharding import Mesh
from jax.sharding import PartitionSpec as P

HEAD = 128
EXTRA = 5
CAP = 81
LIVE_ROWS = 336
MERGE_PAD = 336

norm_eps = 1e-06

DP_AXES = ("x", "zl", "c")
FSDP_AXES = ("y", "zh")


def layer_norm(raw_rows, ln_gain, ln_bias):
    values = raw_rows.astype(jnp.float32)
    centre = jnp.mean(values, axis=-1, keepdims=True)
    spread = jnp.mean(jnp.square(values - centre), axis=-1, keepdims=True)
    return ((values - centre) * lax.rsqrt(spread + norm_eps) * ln_gain + ln_bias).astype(
        jnp.bfloat16
    )


def row_layout(side_row, offset_row, count):
    row_ids = jnp.arange(count, dtype=jnp.int32)
    lengths = EXTRA + side_row * side_row
    inside = (
        (row_ids[:, None] >= offset_row[None, :])
        & (row_ids[:, None] < (offset_row + lengths)[None, :])
    ).astype(jnp.int32)
    covered = jnp.sum(inside, axis=1)
    image_ids = jnp.arange(side_row.shape[0], dtype=jnp.int32)
    segment = jnp.sum(inside * image_ids[None, :], axis=1) + (1 - covered) * side_row.shape[0]
    first_row = jnp.sum(inside * offset_row[None, :], axis=1)
    side_len = jnp.sum(inside * side_row[None, :], axis=1) + (1 - covered)
    patch_id = row_ids - first_row - EXTRA
    is_patch = (covered == 1) & (patch_id >= 0)
    clipped = jnp.maximum(patch_id, 0)
    across = clipped // side_len
    along = clipped % side_len
    side_float = side_len.astype(jnp.float32)
    coord_one = jnp.where(
        is_patch,
        (2 * across + 1).astype(jnp.float32) / side_float - 1.0,
        jnp.zeros_like(side_float),
    )
    coord_two = jnp.where(
        is_patch, (2 * along + 1).astype(jnp.float32) / side_float - 1.0, jnp.zeros_like(side_float)
    )
    return (segment, coord_one, coord_two)


def rotary_tables(coord_one, coord_two, head_size):
    dims = jnp.arange(head_size, dtype=jnp.int32)
    first_half = dims < head_size // 2
    freq_index = (dims % (head_size // 4)).astype(jnp.float32)
    rates = 3.0 * jnp.power(jnp.ones_like(freq_index) * 1.2, freq_index)
    coords = jnp.where(first_half[None, :], coord_one[:, None], coord_two[:, None])
    angles = coords * rates[None, :]
    return (jnp.cos(angles), jnp.sin(angles))


def rotate(tensor, cosine, sine_tab):
    row_count, head_count, head_size = tensor.shape
    quarters = tensor.reshape(row_count, head_count, 2, 2, head_size // 4)
    turned = jnp.stack([-quarters[:, :, :, 1], quarters[:, :, :, 0]], axis=3).reshape(tensor.shape)
    return tensor * cosine[:, None, :] + turned * sine_tab[:, None, :]


def softmax_rounded(scores):
    top = jnp.max(scores, axis=-1, keepdims=True)
    expo = jnp.exp(scores - top)
    return (expo / jnp.sum(expo, axis=-1, keepdims=True)).astype(jnp.bfloat16)


def merge_rows(side_len, offset):
    slot = jnp.arange(CAP, dtype=jnp.int32)
    half_side = side_len // 2
    across = slot // half_side
    along = slot % half_side
    valid = slot < half_side * half_side
    corner = jnp.arange(4, dtype=jnp.int32)
    source_rows = (
        offset
        + EXTRA
        + (2 * across[:, None] + corner[None, :] // 2) * side_len
        + 2 * along[:, None]
        + corner[None, :] % 2
    )
    source_rows = jnp.where(valid[:, None], source_rows, jnp.zeros_like(source_rows))
    return source_rows.reshape(CAP * 4), valid


def attention(queries, key_rows, value_rows, segment):
    scores = jnp.einsum(
        "qhd,khd->hqk", queries, key_rows, preferred_element_type=jnp.float32
    ) / math.sqrt(HEAD)
    allowed = segment[None, :, None] == segment[None, None, :]
    scores = jnp.where(allowed, scores, jnp.full_like(scores, -1e30))
    weights = softmax_rounded(scores)
    return jnp.einsum(
        "hqk,khd->qhd", weights, value_rows, preferred_element_type=jnp.float32
    ).astype(jnp.bfloat16)


def swap_pair(array):
    return lax.ppermute(array, "zh", [(0, 1), (1, 0)])


def shift_dp(block, distance):
    count = 1
    for name in DP_AXES:
        count *= lax.axis_size(name)

    def branch(by):
        if by == 0:
            return lambda v: v
        pairs = [(i, (i + by) % count) for i in range(count)]
        return lambda v: lax.ppermute(v, DP_AXES, pairs)

    return lax.switch(distance, [branch(by) for by in range(count)], block)


def body(stream_rows, ln_gain, ln_bias, w_q, w_k, w_v, w_o, scale_ls, sides, offsets, owners):
    head_cols = w_q.shape[1]
    local_heads = head_cols // HEAD
    side_row = sides[0]
    offset_row = offsets[0]
    feat_cols = scale_ls.shape[0]

    zh = lax.axis_index("zh")
    block = stream_rows.shape[0]
    cut = block // 2
    gathered = []
    for part in (stream_rows[:cut], stream_rows[cut:]):
        other = swap_pair(part)
        pair = jnp.concatenate(
            [jnp.where(zh == 0, part, other), jnp.where(zh == 0, other, part)], axis=0
        )
        stacked = lax.all_gather(pair, "y", axis=0, tiled=False)
        gathered.append(stacked.reshape(stacked.shape[0], 2, cut, stacked.shape[-1]))
    live_rows = jnp.stack(gathered, axis=2).reshape(-1, stream_rows.shape[1])[:LIVE_ROWS]
    normed = layer_norm(live_rows, ln_gain, ln_bias)

    projected = jnp.concatenate(
        [
            jnp.dot(normed, w_q, preferred_element_type=jnp.float32),
            jnp.dot(normed, w_k, preferred_element_type=jnp.float32),
            jnp.dot(normed, w_v, preferred_element_type=jnp.float32),
        ],
        axis=1,
    )
    segment, coord_one, coord_two = row_layout(side_row, offset_row, LIVE_ROWS)
    cosine, sine_tab = rotary_tables(coord_one, coord_two, HEAD)
    queries = rotate(
        projected[:, :head_cols].reshape(LIVE_ROWS, local_heads, HEAD), cosine, sine_tab
    ).astype(jnp.bfloat16)
    key_rows = rotate(
        projected[:, head_cols : 2 * head_cols].reshape(LIVE_ROWS, local_heads, HEAD),
        cosine,
        sine_tab,
    ).astype(jnp.bfloat16)
    value_rows = (
        projected[:, 2 * head_cols :].astype(jnp.bfloat16).reshape(LIVE_ROWS, local_heads, HEAD)
    )
    attended = attention(queries, key_rows, value_rows, segment).reshape(LIVE_ROWS, head_cols)

    source_rows, valid = merge_rows(side_row[0], offset_row[0])
    padded_rows = jnp.concatenate(
        [source_rows, jnp.zeros((MERGE_PAD - source_rows.shape[0],), jnp.int32)]
    )
    merged_attended = jnp.take(attended, padded_rows, axis=0)
    partial_sum = jnp.dot(merged_attended, w_o, preferred_element_type=jnp.float32).astype(
        jnp.bfloat16
    )
    half = MERGE_PAD // 2
    sums = []
    for part in (partial_sum[:half], partial_sum[half:]):
        quarter = lax.psum_scatter(part, "y", scatter_dimension=1, tiled=True)
        split = quarter.reshape(half, 2, feat_cols)
        mine = jnp.where(zh == 0, split[:, 0], split[:, 1])
        theirs = jnp.where(zh == 0, split[:, 1], split[:, 0])
        sums.append(mine.astype(jnp.float32) + swap_pair(theirs).astype(jnp.float32))
    branch = jnp.concatenate(sums, axis=0)[: source_rows.shape[0]]

    feat_index = lax.axis_index("y") * lax.axis_size("zh") + zh
    residual = jnp.take(
        lax.dynamic_slice_in_dim(live_rows, feat_index * feat_cols, feat_cols, axis=1),
        source_rows,
        axis=0,
    )
    updated = (residual.astype(jnp.float32) + scale_ls * branch).astype(jnp.bfloat16)
    merged = jnp.where(
        jnp.repeat(valid, 4)[:, None], updated, jnp.zeros_like(updated)
    ).reshape(1, CAP, 4, feat_cols)

    group_count = 1
    for name in DP_AXES:
        group_count *= lax.axis_size(name)
    distance = owners[0, 0] % group_count
    delivered = shift_dp(merged, distance)
    return delivered[None]


def solution(mesh):
    dp_size, fsdp_size = mesh.devices.shape
    split_mesh = Mesh(
        np.asarray(mesh.devices).reshape(4, dp_size // 8, 2, fsdp_size // 2, 2),
        DP_AXES + FSDP_AXES,
    )
    rows = DP_AXES + FSDP_AXES
    return jax.shard_map(
        body,
        mesh=split_mesh,
        in_specs=(
            P(rows, None),
            P(),
            P(),
            P(None, FSDP_AXES),
            P(None, FSDP_AXES),
            P(None, FSDP_AXES),
            P(FSDP_AXES, None),
            P(FSDP_AXES),
            P(DP_AXES, None),
            P(DP_AXES, None),
            P(),
        ),
        out_specs=P(DP_AXES, None, None, None, FSDP_AXES),
        check_vma=False,
    )
```

```python
import math

import jax
import jax.numpy as jnp
import numpy as np
from jax import lax
from jax.sharding import Mesh
from jax.sharding import PartitionSpec as P

HEAD = 128
EXTRA = 5
CAP = 81
LIVE_ROWS = 336
MERGE_PAD = 328

norm_eps = 1e-06

DP_AXES = ("x", "zl", "c")
FSDP_AXES = ("y", "zh")


def layer_norm(raw_rows, ln_gain, ln_bias):
    values = raw_rows.astype(jnp.float32)
    centre = jnp.mean(values, axis=-1, keepdims=True)
    spread = jnp.mean(jnp.square(values - centre), axis=-1, keepdims=True)
    return ((values - centre) * lax.rsqrt(spread + norm_eps) * ln_gain + ln_bias).astype(
        jnp.bfloat16
    )


def row_layout(side_row, offset_row, count):
    row_ids = jnp.arange(count, dtype=jnp.int32)
    lengths = EXTRA + side_row * side_row
    inside = (
        (row_ids[:, None] >= offset_row[None, :])
        & (row_ids[:, None] < (offset_row + lengths)[None, :])
    ).astype(jnp.int32)
    covered = jnp.sum(inside, axis=1)
    image_ids = jnp.arange(side_row.shape[0], dtype=jnp.int32)
    segment = jnp.sum(inside * image_ids[None, :], axis=1) + (1 - covered) * side_row.shape[0]
    first_row = jnp.sum(inside * offset_row[None, :], axis=1)
    side_len = jnp.sum(inside * side_row[None, :], axis=1) + (1 - covered)
    patch_id = row_ids - first_row - EXTRA
    is_patch = (covered == 1) & (patch_id >= 0)
    clipped = jnp.maximum(patch_id, 0)
    across = clipped // side_len
    along = clipped % side_len
    side_float = side_len.astype(jnp.float32)
    coord_one = jnp.where(
        is_patch,
        (2 * across + 1).astype(jnp.float32) / side_float - 1.0,
        jnp.zeros_like(side_float),
    )
    coord_two = jnp.where(
        is_patch, (2 * along + 1).astype(jnp.float32) / side_float - 1.0, jnp.zeros_like(side_float)
    )
    return (segment, coord_one, coord_two)


def rotary_tables(coord_one, coord_two, head_size):
    dims = jnp.arange(head_size, dtype=jnp.int32)
    first_half = dims < head_size // 2
    freq_index = (dims % (head_size // 4)).astype(jnp.float32)
    rates = 3.0 * jnp.power(jnp.ones_like(freq_index) * 1.2, freq_index)
    coords = jnp.where(first_half[None, :], coord_one[:, None], coord_two[:, None])
    angles = coords * rates[None, :]
    return (jnp.cos(angles), jnp.sin(angles))


def rotate(tensor, cosine, sine_tab):
    row_count, head_count, head_size = tensor.shape
    quarters = tensor.reshape(row_count, head_count, 2, 2, head_size // 4)
    turned = jnp.stack([-quarters[:, :, :, 1], quarters[:, :, :, 0]], axis=3).reshape(tensor.shape)
    return tensor * cosine[:, None, :] + turned * sine_tab[:, None, :]


def softmax_rounded(scores):
    top = jnp.max(scores, axis=-1, keepdims=True)
    expo = jnp.exp(scores - top)
    return (expo / jnp.sum(expo, axis=-1, keepdims=True)).astype(jnp.bfloat16)


def merge_rows(side_len, offset):
    slot = jnp.arange(CAP, dtype=jnp.int32)
    half_side = side_len // 2
    across = slot // half_side
    along = slot % half_side
    valid = slot < half_side * half_side
    corner = jnp.arange(4, dtype=jnp.int32)
    source_rows = (
        offset
        + EXTRA
        + (2 * across[:, None] + corner[None, :] // 2) * side_len
        + 2 * along[:, None]
        + corner[None, :] % 2
    )
    source_rows = jnp.where(valid[:, None], source_rows, jnp.zeros_like(source_rows))
    return source_rows.reshape(CAP * 4), valid


def attention(queries, key_rows, value_rows, segment):
    scores = jnp.einsum(
        "qhd,khd->hqk", queries, key_rows, preferred_element_type=jnp.float32
    ) / math.sqrt(HEAD)
    allowed = segment[None, :, None] == segment[None, None, :]
    scores = jnp.where(allowed, scores, jnp.full_like(scores, -1e30))
    weights = softmax_rounded(scores)
    return jnp.einsum(
        "hqk,khd->qhd", weights, value_rows, preferred_element_type=jnp.float32
    ).astype(jnp.bfloat16)


def swap_pair(array):
    return lax.ppermute(array, "zh", [(0, 1), (1, 0)])


def shift_dp(block, distance):
    count = 1
    for name in DP_AXES:
        count *= lax.axis_size(name)

    def branch(by):
        if by == 0:
            return lambda v: v
        pairs = [(i, (i + by) % count) for i in range(count)]
        return lambda v: lax.ppermute(v, DP_AXES, pairs)

    return lax.switch(distance, [branch(by) for by in range(count)], block)


def body(stream_rows, ln_gain, ln_bias, w_q, w_k, w_v, w_o, scale_ls, sides, offsets, owners):
    head_cols = w_q.shape[1]
    local_heads = head_cols // HEAD
    side_row = sides[0]
    offset_row = offsets[0]
    feat_cols = scale_ls.shape[0]

    zh = lax.axis_index("zh")
    other = swap_pair(stream_rows)
    pair = jnp.concatenate(
        [jnp.where(zh == 0, stream_rows, other), jnp.where(zh == 0, other, stream_rows)], axis=0
    )
    live_rows = lax.all_gather(pair, "y", axis=0, tiled=True)[:LIVE_ROWS]
    normed = layer_norm(live_rows, ln_gain, ln_bias)

    projected = jnp.concatenate(
        [
            jnp.dot(normed, w_q, preferred_element_type=jnp.float32),
            jnp.dot(normed, w_k, preferred_element_type=jnp.float32),
            jnp.dot(normed, w_v, preferred_element_type=jnp.float32),
        ],
        axis=1,
    )
    segment, coord_one, coord_two = row_layout(side_row, offset_row, LIVE_ROWS)
    cosine, sine_tab = rotary_tables(coord_one, coord_two, HEAD)
    queries = rotate(
        projected[:, :head_cols].reshape(LIVE_ROWS, local_heads, HEAD), cosine, sine_tab
    ).astype(jnp.bfloat16)
    key_rows = rotate(
        projected[:, head_cols : 2 * head_cols].reshape(LIVE_ROWS, local_heads, HEAD),
        cosine,
        sine_tab,
    ).astype(jnp.bfloat16)
    value_rows = (
        projected[:, 2 * head_cols :].astype(jnp.bfloat16).reshape(LIVE_ROWS, local_heads, HEAD)
    )
    attended = attention(queries, key_rows, value_rows, segment).reshape(LIVE_ROWS, head_cols)

    source_rows, valid = merge_rows(side_row[0], offset_row[0])
    padded_rows = jnp.concatenate(
        [source_rows, jnp.zeros((MERGE_PAD - source_rows.shape[0],), jnp.int32)]
    )
    merged_attended = jnp.take(attended, padded_rows, axis=0)
    partial_sum = jnp.dot(merged_attended, w_o, preferred_element_type=jnp.float32).astype(
        jnp.bfloat16
    )
    quarter = lax.psum_scatter(partial_sum, "y", scatter_dimension=1, tiled=True)
    split = quarter.reshape(MERGE_PAD, 2, feat_cols)
    mine = jnp.where(zh == 0, split[:, 0], split[:, 1])
    theirs = jnp.where(zh == 0, split[:, 1], split[:, 0])
    branch = (mine.astype(jnp.float32) + swap_pair(theirs).astype(jnp.float32))[
        : source_rows.shape[0]
    ]

    feat_index = lax.axis_index("y") * lax.axis_size("zh") + zh
    residual = jnp.take(
        lax.dynamic_slice_in_dim(live_rows, feat_index * feat_cols, feat_cols, axis=1),
        source_rows,
        axis=0,
    )
    updated = (residual.astype(jnp.float32) + scale_ls * branch).astype(jnp.bfloat16)
    merged = jnp.where(
        jnp.repeat(valid, 4)[:, None], updated, jnp.zeros_like(updated)
    ).reshape(1, CAP, 4, feat_cols)

    group_count = 1
    for name in DP_AXES:
        group_count *= lax.axis_size(name)
    distance = owners[0, 0] % group_count
    delivered = shift_dp(merged, distance)
    return delivered[None]


def solution(mesh):
    dp_size, fsdp_size = mesh.devices.shape
    split_mesh = Mesh(
        np.asarray(mesh.devices).reshape(4, dp_size // 8, 2, fsdp_size // 2, 2),
        DP_AXES + FSDP_AXES,
    )
    rows = DP_AXES + FSDP_AXES
    return jax.shard_map(
        body,
        mesh=split_mesh,
        in_specs=(
            P(rows, None),
            P(),
            P(),
            P(None, FSDP_AXES),
            P(None, FSDP_AXES),
            P(None, FSDP_AXES),
            P(FSDP_AXES, None),
            P(FSDP_AXES),
            P(DP_AXES, None),
            P(DP_AXES, None),
            P(),
        ),
        out_specs=P(DP_AXES, None, None, None, FSDP_AXES),
        check_vma=False,
    )
```

```python
import math

import jax
import jax.numpy as jnp
import numpy as np
from jax import lax
from jax.sharding import Mesh
from jax.sharding import PartitionSpec as P

HEAD = 128
EXTRA = 5
CAP = 81
LIVE_ROWS = 336
MERGE_PAD = 328

norm_eps = 1e-06

DP_AXES = ("x", "zl", "c")
FSDP_AXES = ("y", "zh")


def layer_norm(raw_rows, ln_gain, ln_bias):
    values = raw_rows.astype(jnp.float32)
    centre = jnp.mean(values, axis=-1, keepdims=True)
    spread = jnp.mean(jnp.square(values - centre), axis=-1, keepdims=True)
    return ((values - centre) * lax.rsqrt(spread + norm_eps) * ln_gain + ln_bias).astype(
        jnp.bfloat16
    )


def row_layout(side_row, offset_row, count):
    row_ids = jnp.arange(count, dtype=jnp.int32)
    lengths = EXTRA + side_row * side_row
    inside = (
        (row_ids[:, None] >= offset_row[None, :])
        & (row_ids[:, None] < (offset_row + lengths)[None, :])
    ).astype(jnp.int32)
    covered = jnp.sum(inside, axis=1)
    image_ids = jnp.arange(side_row.shape[0], dtype=jnp.int32)
    segment = jnp.sum(inside * image_ids[None, :], axis=1) + (1 - covered) * side_row.shape[0]
    first_row = jnp.sum(inside * offset_row[None, :], axis=1)
    side_len = jnp.sum(inside * side_row[None, :], axis=1) + (1 - covered)
    patch_id = row_ids - first_row - EXTRA
    is_patch = (covered == 1) & (patch_id >= 0)
    clipped = jnp.maximum(patch_id, 0)
    across = clipped // side_len
    along = clipped % side_len
    side_float = side_len.astype(jnp.float32)
    coord_one = jnp.where(
        is_patch,
        (2 * across + 1).astype(jnp.float32) / side_float - 1.0,
        jnp.zeros_like(side_float),
    )
    coord_two = jnp.where(
        is_patch, (2 * along + 1).astype(jnp.float32) / side_float - 1.0, jnp.zeros_like(side_float)
    )
    return (segment, coord_one, coord_two)


def rotary_tables(coord_one, coord_two, head_size):
    dims = jnp.arange(head_size, dtype=jnp.int32)
    first_half = dims < head_size // 2
    freq_index = (dims % (head_size // 4)).astype(jnp.float32)
    rates = 3.0 * jnp.power(jnp.ones_like(freq_index) * 1.2, freq_index)
    coords = jnp.where(first_half[None, :], coord_one[:, None], coord_two[:, None])
    angles = coords * rates[None, :]
    return (jnp.cos(angles), jnp.sin(angles))


def rotate(tensor, cosine, sine_tab):
    row_count, head_count, head_size = tensor.shape
    quarters = tensor.reshape(row_count, head_count, 2, 2, head_size // 4)
    turned = jnp.stack([-quarters[:, :, :, 1], quarters[:, :, :, 0]], axis=3).reshape(tensor.shape)
    return tensor * cosine[:, None, :] + turned * sine_tab[:, None, :]


def softmax_rounded(scores):
    top = jnp.max(scores, axis=-1, keepdims=True)
    expo = jnp.exp(scores - top)
    return (expo / jnp.sum(expo, axis=-1, keepdims=True)).astype(jnp.bfloat16)


def merge_rows(side_len, offset):
    slot = jnp.arange(CAP, dtype=jnp.int32)
    half_side = side_len // 2
    across = slot // half_side
    along = slot % half_side
    valid = slot < half_side * half_side
    corner = jnp.arange(4, dtype=jnp.int32)
    source_rows = (
        offset
        + EXTRA
        + (2 * across[:, None] + corner[None, :] // 2) * side_len
        + 2 * along[:, None]
        + corner[None, :] % 2
    )
    source_rows = jnp.where(valid[:, None], source_rows, jnp.zeros_like(source_rows))
    return source_rows.reshape(CAP * 4), valid


def attention(queries, key_rows, value_rows, segment):
    scores = jnp.einsum(
        "qhd,khd->hqk", queries, key_rows, preferred_element_type=jnp.float32
    ) / math.sqrt(HEAD)
    allowed = segment[None, :, None] == segment[None, None, :]
    scores = jnp.where(allowed, scores, jnp.full_like(scores, -1e30))
    weights = softmax_rounded(scores)
    return jnp.einsum(
        "hqk,khd->qhd", weights, value_rows, preferred_element_type=jnp.float32
    ).astype(jnp.bfloat16)


def one_hot(rows, count):
    return (rows[:, None] == jnp.arange(count, dtype=jnp.int32)[None, :]).astype(jnp.bfloat16)


def swap_pair(array):
    return lax.ppermute(array, "zh", [(0, 1), (1, 0)])


def shift_dp(block, distance):
    count = 1
    for name in DP_AXES:
        count *= lax.axis_size(name)

    def branch(by):
        if by == 0:
            return lambda v: v
        pairs = [(i, (i + by) % count) for i in range(count)]
        return lambda v: lax.ppermute(v, DP_AXES, pairs)

    return lax.switch(distance, [branch(by) for by in range(count)], block)


def body(stream_rows, ln_gain, ln_bias, w_q, w_k, w_v, w_o, scale_ls, sides, offsets, owners):
    head_cols = w_q.shape[1]
    local_heads = head_cols // HEAD
    side_row = sides[0]
    offset_row = offsets[0]
    feat_cols = scale_ls.shape[0]

    zh = lax.axis_index("zh")
    own_blocks = lax.all_gather(stream_rows, "y", axis=0, tiled=False)
    partner_blocks = lax.all_gather(swap_pair(stream_rows), "y", axis=0, tiled=False)
    live_rows = jnp.where(
        zh == 0,
        jnp.stack([own_blocks, partner_blocks], axis=1),
        jnp.stack([partner_blocks, own_blocks], axis=1),
    ).reshape(-1, stream_rows.shape[1])[:LIVE_ROWS]
    normed = layer_norm(live_rows, ln_gain, ln_bias)

    projected = jnp.concatenate(
        [
            jnp.dot(normed, w_q, preferred_element_type=jnp.float32),
            jnp.dot(normed, w_k, preferred_element_type=jnp.float32),
            jnp.dot(normed, w_v, preferred_element_type=jnp.float32),
        ],
        axis=1,
    )
    segment, coord_one, coord_two = row_layout(side_row, offset_row, LIVE_ROWS)
    cosine, sine_tab = rotary_tables(coord_one, coord_two, HEAD)
    queries = rotate(
        projected[:, :head_cols].reshape(LIVE_ROWS, local_heads, HEAD), cosine, sine_tab
    ).astype(jnp.bfloat16)
    key_rows = rotate(
        projected[:, head_cols : 2 * head_cols].reshape(LIVE_ROWS, local_heads, HEAD),
        cosine,
        sine_tab,
    ).astype(jnp.bfloat16)
    value_rows = (
        projected[:, 2 * head_cols :].astype(jnp.bfloat16).reshape(LIVE_ROWS, local_heads, HEAD)
    )
    attended = attention(queries, key_rows, value_rows, segment).reshape(LIVE_ROWS, head_cols)

    source_rows, valid = merge_rows(side_row[0], offset_row[0])
    padded_rows = jnp.concatenate(
        [source_rows, jnp.zeros((MERGE_PAD - source_rows.shape[0],), jnp.int32)]
    )
    merged_attended = jnp.dot(
        one_hot(padded_rows, LIVE_ROWS), attended, preferred_element_type=jnp.float32
    ).astype(jnp.bfloat16)
    partial_sum = jnp.dot(merged_attended, w_o, preferred_element_type=jnp.float32).astype(
        jnp.bfloat16
    )
    quarter = lax.psum_scatter(partial_sum, "y", scatter_dimension=1, tiled=True)
    split = quarter.reshape(MERGE_PAD, 2, feat_cols)
    mine = jnp.where(zh == 0, split[:, 0], split[:, 1])
    theirs = jnp.where(zh == 0, split[:, 1], split[:, 0])
    branch = (mine.astype(jnp.float32) + swap_pair(theirs).astype(jnp.float32))[
        : source_rows.shape[0]
    ]

    feat_index = lax.axis_index("y") * lax.axis_size("zh") + zh
    residual = jnp.dot(
        one_hot(source_rows, LIVE_ROWS),
        lax.dynamic_slice_in_dim(live_rows, feat_index * feat_cols, feat_cols, axis=1),
        preferred_element_type=jnp.float32,
    )
    updated = (residual.astype(jnp.float32) + scale_ls * branch).astype(jnp.bfloat16)
    merged = jnp.where(
        jnp.repeat(valid, 4)[:, None], updated, jnp.zeros_like(updated)
    ).reshape(1, CAP, 4, feat_cols)

    group_count = 1
    for name in DP_AXES:
        group_count *= lax.axis_size(name)
    distance = owners[0, 0] % group_count
    delivered = shift_dp(merged, distance)
    return delivered[None]


def solution(mesh):
    dp_size, fsdp_size = mesh.devices.shape
    split_mesh = Mesh(
        np.asarray(mesh.devices).reshape(4, dp_size // 8, 2, fsdp_size // 2, 2),
        DP_AXES + FSDP_AXES,
    )
    rows = DP_AXES + FSDP_AXES
    return jax.shard_map(
        body,
        mesh=split_mesh,
        in_specs=(
            P(rows, None),
            P(),
            P(),
            P(None, FSDP_AXES),
            P(None, FSDP_AXES),
            P(None, FSDP_AXES),
            P(FSDP_AXES, None),
            P(FSDP_AXES),
            P(DP_AXES, None),
            P(DP_AXES, None),
            P(),
        ),
        out_specs=P(DP_AXES, None, None, None, FSDP_AXES),
        check_vma=False,
    )
```

```python
import math

import jax
import jax.numpy as jnp
import numpy as np
from jax import lax
from jax.sharding import Mesh
from jax.sharding import PartitionSpec as P

HEAD = 128
EXTRA = 5
CAP = 81
LIVE_ROWS = 336
MERGE_PAD = 328

norm_eps = 1e-06

DP_AXES = ("x", "zl", "c")
FSDP_AXES = ("y", "zh")


def layer_norm(raw_rows, ln_gain, ln_bias):
    values = raw_rows.astype(jnp.float32)
    centre = jnp.mean(values, axis=-1, keepdims=True)
    spread = jnp.mean(jnp.square(values - centre), axis=-1, keepdims=True)
    return ((values - centre) * lax.rsqrt(spread + norm_eps) * ln_gain + ln_bias).astype(
        jnp.bfloat16
    )


def row_layout(side_row, offset_row, count):
    row_ids = jnp.arange(count, dtype=jnp.int32)
    lengths = EXTRA + side_row * side_row
    inside = (
        (row_ids[:, None] >= offset_row[None, :])
        & (row_ids[:, None] < (offset_row + lengths)[None, :])
    ).astype(jnp.int32)
    covered = jnp.sum(inside, axis=1)
    image_ids = jnp.arange(side_row.shape[0], dtype=jnp.int32)
    segment = jnp.sum(inside * image_ids[None, :], axis=1) + (1 - covered) * side_row.shape[0]
    first_row = jnp.sum(inside * offset_row[None, :], axis=1)
    side_len = jnp.sum(inside * side_row[None, :], axis=1) + (1 - covered)
    patch_id = row_ids - first_row - EXTRA
    is_patch = (covered == 1) & (patch_id >= 0)
    clipped = jnp.maximum(patch_id, 0)
    across = clipped // side_len
    along = clipped % side_len
    side_float = side_len.astype(jnp.float32)
    coord_one = jnp.where(
        is_patch,
        (2 * across + 1).astype(jnp.float32) / side_float - 1.0,
        jnp.zeros_like(side_float),
    )
    coord_two = jnp.where(
        is_patch, (2 * along + 1).astype(jnp.float32) / side_float - 1.0, jnp.zeros_like(side_float)
    )
    return (segment, coord_one, coord_two)


def rotary_tables(coord_one, coord_two, head_size):
    dims = jnp.arange(head_size, dtype=jnp.int32)
    first_half = dims < head_size // 2
    freq_index = (dims % (head_size // 4)).astype(jnp.float32)
    rates = 3.0 * jnp.power(jnp.ones_like(freq_index) * 1.2, freq_index)
    coords = jnp.where(first_half[None, :], coord_one[:, None], coord_two[:, None])
    angles = coords * rates[None, :]
    return (jnp.cos(angles), jnp.sin(angles))


def rotate(tensor, cosine, sine_tab):
    row_count, head_count, head_size = tensor.shape
    quarters = tensor.reshape(row_count, head_count, 2, 2, head_size // 4)
    turned = jnp.stack([-quarters[:, :, :, 1], quarters[:, :, :, 0]], axis=3).reshape(tensor.shape)
    return tensor * cosine[:, None, :] + turned * sine_tab[:, None, :]


def softmax_rounded(scores):
    top = jnp.max(scores, axis=-1, keepdims=True)
    expo = jnp.exp(scores - top)
    return (expo / jnp.sum(expo, axis=-1, keepdims=True)).astype(jnp.bfloat16)


def merge_rows(side_len, offset):
    slot = jnp.arange(CAP, dtype=jnp.int32)
    half_side = side_len // 2
    across = slot // half_side
    along = slot % half_side
    valid = slot < half_side * half_side
    corner = jnp.arange(4, dtype=jnp.int32)
    source_rows = (
        offset
        + EXTRA
        + (2 * across[:, None] + corner[None, :] // 2) * side_len
        + 2 * along[:, None]
        + corner[None, :] % 2
    )
    source_rows = jnp.where(valid[:, None], source_rows, jnp.zeros_like(source_rows))
    return source_rows.reshape(CAP * 4), valid


def attention(queries, key_rows, value_rows, segment):
    scores = jnp.einsum(
        "qhd,khd->hqk", queries, key_rows, preferred_element_type=jnp.float32
    ) / math.sqrt(HEAD)
    allowed = segment[None, :, None] == segment[None, None, :]
    scores = jnp.where(allowed, scores, jnp.full_like(scores, -1e30))
    weights = softmax_rounded(scores)
    return jnp.einsum(
        "hqk,khd->qhd", weights, value_rows, preferred_element_type=jnp.float32
    ).astype(jnp.bfloat16)


def one_hot(rows, count):
    return (rows[:, None] == jnp.arange(count, dtype=jnp.int32)[None, :]).astype(jnp.bfloat16)


def swap_pair(array):
    return lax.ppermute(array, "zh", [(0, 1), (1, 0)])


def shift_dp(block, distance):
    count = 1
    for name in DP_AXES:
        count *= lax.axis_size(name)

    def branch(by):
        if by == 0:
            return lambda v: v
        pairs = [(i, (i + by) % count) for i in range(count)]
        return lambda v: lax.ppermute(v, DP_AXES, pairs)

    return lax.switch(distance, [branch(by) for by in range(count)], block)


def deliver_halves(mine, theirs, distance):
    count = 1
    for name in DP_AXES:
        count *= lax.axis_size(name)

    def branch(by):
        if by == 0:
            return lambda a, b: (a, swap_pair(b))
        same = [(i, (i + by) % count) for i in range(count)]
        across = [
            (2 * i + h, 2 * ((i + by) % count) + 1 - h) for i in range(count) for h in range(2)
        ]
        return lambda a, b: (
            lax.ppermute(a, DP_AXES, same),
            lax.ppermute(b, DP_AXES + ("zh",), across),
        )

    return lax.switch(distance, [branch(by) for by in range(count)], mine, theirs)


def body(stream_rows, ln_gain, ln_bias, w_q, w_k, w_v, w_o, scale_ls, sides, offsets, owners):
    head_cols = w_q.shape[1]
    local_heads = head_cols // HEAD
    side_row = sides[0]
    offset_row = offsets[0]
    feat_cols = scale_ls.shape[0]

    zh = lax.axis_index("zh")
    own_blocks = lax.all_gather(stream_rows, "y", axis=0, tiled=False)
    partner_blocks = lax.all_gather(swap_pair(stream_rows), "y", axis=0, tiled=False)
    live_rows = jnp.where(
        zh == 0,
        jnp.stack([own_blocks, partner_blocks], axis=1),
        jnp.stack([partner_blocks, own_blocks], axis=1),
    ).reshape(-1, stream_rows.shape[1])[:LIVE_ROWS]
    normed = layer_norm(live_rows, ln_gain, ln_bias)

    projected = jnp.concatenate(
        [
            jnp.dot(normed, w_q, preferred_element_type=jnp.float32),
            jnp.dot(normed, w_k, preferred_element_type=jnp.float32),
            jnp.dot(normed, w_v, preferred_element_type=jnp.float32),
        ],
        axis=1,
    )
    segment, coord_one, coord_two = row_layout(side_row, offset_row, LIVE_ROWS)
    cosine, sine_tab = rotary_tables(coord_one, coord_two, HEAD)
    queries = rotate(
        projected[:, :head_cols].reshape(LIVE_ROWS, local_heads, HEAD), cosine, sine_tab
    ).astype(jnp.bfloat16)
    key_rows = rotate(
        projected[:, head_cols : 2 * head_cols].reshape(LIVE_ROWS, local_heads, HEAD),
        cosine,
        sine_tab,
    ).astype(jnp.bfloat16)
    value_rows = (
        projected[:, 2 * head_cols :].astype(jnp.bfloat16).reshape(LIVE_ROWS, local_heads, HEAD)
    )
    attended = attention(queries, key_rows, value_rows, segment).reshape(LIVE_ROWS, head_cols)

    source_rows, valid = merge_rows(side_row[0], offset_row[0])
    padded_rows = jnp.concatenate(
        [source_rows, jnp.zeros((MERGE_PAD - source_rows.shape[0],), jnp.int32)]
    )
    merged_attended = jnp.dot(
        one_hot(padded_rows, LIVE_ROWS), attended, preferred_element_type=jnp.float32
    ).astype(jnp.bfloat16)
    partial_sum = jnp.dot(merged_attended, w_o, preferred_element_type=jnp.float32).astype(
        jnp.bfloat16
    )
    group_count = 1
    for name in DP_AXES:
        group_count *= lax.axis_size(name)
    distance = owners[0, 0] % group_count

    feat_index = lax.axis_index("y") * lax.axis_size("zh") + zh
    keep = jnp.repeat(valid, 4)[:, None]
    residual = jnp.dot(
        one_hot(source_rows, LIVE_ROWS),
        lax.dynamic_slice_in_dim(live_rows, feat_index * feat_cols, feat_cols, axis=1),
        preferred_element_type=jnp.float32,
    ).astype(jnp.bfloat16)
    residual = shift_dp(jnp.where(keep, residual, jnp.zeros_like(residual)), distance)

    quarter = lax.psum_scatter(partial_sum, "y", scatter_dimension=1, tiled=True)
    split = quarter.reshape(MERGE_PAD, 2, feat_cols)[: source_rows.shape[0]]
    mine = jnp.where(zh == 0, split[:, 0], split[:, 1])
    theirs = jnp.where(zh == 0, split[:, 1], split[:, 0])
    mine = jnp.where(keep, mine, jnp.zeros_like(mine))
    theirs = jnp.where(keep, theirs, jnp.zeros_like(theirs))
    mine, theirs = deliver_halves(mine, theirs, distance)
    branch = mine.astype(jnp.float32) + theirs.astype(jnp.float32)
    updated = (residual.astype(jnp.float32) + scale_ls * branch).astype(jnp.bfloat16)
    delivered = updated.reshape(1, CAP, 4, feat_cols)
    return delivered[None]


def solution(mesh):
    dp_size, fsdp_size = mesh.devices.shape
    split_mesh = Mesh(
        np.asarray(mesh.devices).reshape(4, dp_size // 8, 2, fsdp_size // 2, 2),
        DP_AXES + FSDP_AXES,
    )
    rows = DP_AXES + FSDP_AXES
    return jax.shard_map(
        body,
        mesh=split_mesh,
        in_specs=(
            P(rows, None),
            P(),
            P(),
            P(None, FSDP_AXES),
            P(None, FSDP_AXES),
            P(None, FSDP_AXES),
            P(FSDP_AXES, None),
            P(FSDP_AXES),
            P(DP_AXES, None),
            P(DP_AXES, None),
            P(),
        ),
        out_specs=P(DP_AXES, None, None, None, FSDP_AXES),
        check_vma=False,
    )
```

```python
import math

import jax
import jax.numpy as jnp
import numpy as np
from jax import lax
from jax.sharding import Mesh
from jax.sharding import PartitionSpec as P

HEAD = 128
EXTRA = 5
CAP = 81
LIVE_ROWS = 336
MERGE_PAD = 328

norm_eps = 1e-06

DP_AXES = ("x", "zl", "c")
FSDP_AXES = ("y", "zh")


def layer_norm(raw_rows, ln_gain, ln_bias):
    values = raw_rows.astype(jnp.float32)
    centre = jnp.mean(values, axis=-1, keepdims=True)
    spread = jnp.mean(jnp.square(values - centre), axis=-1, keepdims=True)
    return ((values - centre) * lax.rsqrt(spread + norm_eps) * ln_gain + ln_bias).astype(
        jnp.bfloat16
    )


def row_layout(side_row, offset_row, count):
    row_ids = jnp.arange(count, dtype=jnp.int32)
    lengths = EXTRA + side_row * side_row
    inside = (
        (row_ids[:, None] >= offset_row[None, :])
        & (row_ids[:, None] < (offset_row + lengths)[None, :])
    ).astype(jnp.int32)
    covered = jnp.sum(inside, axis=1)
    image_ids = jnp.arange(side_row.shape[0], dtype=jnp.int32)
    segment = jnp.sum(inside * image_ids[None, :], axis=1) + (1 - covered) * side_row.shape[0]
    first_row = jnp.sum(inside * offset_row[None, :], axis=1)
    side_len = jnp.sum(inside * side_row[None, :], axis=1) + (1 - covered)
    patch_id = row_ids - first_row - EXTRA
    is_patch = (covered == 1) & (patch_id >= 0)
    clipped = jnp.maximum(patch_id, 0)
    across = clipped // side_len
    along = clipped % side_len
    side_float = side_len.astype(jnp.float32)
    coord_one = jnp.where(
        is_patch,
        (2 * across + 1).astype(jnp.float32) / side_float - 1.0,
        jnp.zeros_like(side_float),
    )
    coord_two = jnp.where(
        is_patch, (2 * along + 1).astype(jnp.float32) / side_float - 1.0, jnp.zeros_like(side_float)
    )
    return (segment, coord_one, coord_two)


def rotary_tables(coord_one, coord_two, head_size):
    dims = jnp.arange(head_size, dtype=jnp.int32)
    first_half = dims < head_size // 2
    freq_index = (dims % (head_size // 4)).astype(jnp.float32)
    rates = 3.0 * jnp.power(jnp.ones_like(freq_index) * 1.2, freq_index)
    coords = jnp.where(first_half[None, :], coord_one[:, None], coord_two[:, None])
    angles = coords * rates[None, :]
    return (jnp.cos(angles), jnp.sin(angles))


def rotate(tensor, cosine, sine_tab):
    row_count, head_count, head_size = tensor.shape
    quarters = tensor.reshape(row_count, head_count, 2, 2, head_size // 4)
    turned = jnp.stack([-quarters[:, :, :, 1], quarters[:, :, :, 0]], axis=3).reshape(tensor.shape)
    return tensor * cosine[:, None, :] + turned * sine_tab[:, None, :]


def softmax_rounded(scores):
    top = jnp.max(scores, axis=-1, keepdims=True)
    expo = jnp.exp(scores - top)
    return (expo / jnp.sum(expo, axis=-1, keepdims=True)).astype(jnp.bfloat16)


def merge_rows(side_len, offset):
    slot = jnp.arange(CAP, dtype=jnp.int32)
    half_side = side_len // 2
    across = slot // half_side
    along = slot % half_side
    valid = slot < half_side * half_side
    corner = jnp.arange(4, dtype=jnp.int32)
    source_rows = (
        offset
        + EXTRA
        + (2 * across[:, None] + corner[None, :] // 2) * side_len
        + 2 * along[:, None]
        + corner[None, :] % 2
    )
    source_rows = jnp.where(valid[:, None], source_rows, jnp.zeros_like(source_rows))
    return source_rows.reshape(CAP * 4), valid


def attention(queries, key_rows, value_rows, segment):
    scores = jnp.einsum(
        "qhd,khd->hqk", queries, key_rows, preferred_element_type=jnp.float32
    ) / math.sqrt(HEAD)
    allowed = segment[None, :, None] == segment[None, None, :]
    scores = jnp.where(allowed, scores, jnp.full_like(scores, -1e30))
    weights = softmax_rounded(scores)
    return jnp.einsum(
        "hqk,khd->qhd", weights, value_rows, preferred_element_type=jnp.float32
    ).astype(jnp.bfloat16)


def one_hot(rows, count):
    return (rows[:, None] == jnp.arange(count, dtype=jnp.int32)[None, :]).astype(jnp.bfloat16)


def swap_pair(array):
    return lax.ppermute(array, "zh", [(0, 1), (1, 0)])


def shift_dp(block, distance):
    count = 1
    for name in DP_AXES:
        count *= lax.axis_size(name)

    def branch(by):
        if by == 0:
            return lambda v: v
        pairs = [(i, (i + by) % count) for i in range(count)]
        return lambda v: lax.ppermute(v, DP_AXES, pairs)

    return lax.switch(distance, [branch(by) for by in range(count)], block)


def shift_by_exchange(payload, distance, count):
    size = payload.size
    lanes = 128
    rows = -(-size // (count * lanes))
    rows = -(-rows // 16) * 16
    flat = jnp.pad(payload.reshape(-1), (0, count * rows * lanes - size))
    pieces = lax.all_to_all(flat.reshape(count, rows, lanes), DP_AXES, 0, 0, tiled=True)
    rolled = jnp.roll(pieces, distance, axis=0)
    back = lax.all_to_all(rolled, DP_AXES, 0, 0, tiled=True)
    return back.reshape(-1)[:size].reshape(payload.shape)


def deliver_halves(mine, theirs, distance):
    count = 1
    for name in DP_AXES:
        count *= lax.axis_size(name)

    def branch(by):
        if by == 0:
            return lambda a, b: (a, swap_pair(b))
        same = [(i, (i + by) % count) for i in range(count)]
        across = [
            (2 * i + h, 2 * ((i + by) % count) + 1 - h) for i in range(count) for h in range(2)
        ]
        return lambda a, b: (
            lax.ppermute(a, DP_AXES, same),
            lax.ppermute(b, DP_AXES + ("zh",), across),
        )

    return lax.switch(distance, [branch(by) for by in range(count)], mine, theirs)


def body(stream_rows, ln_gain, ln_bias, w_q, w_k, w_v, w_o, scale_ls, sides, offsets, owners):
    head_cols = w_q.shape[1]
    local_heads = head_cols // HEAD
    side_row = sides[0]
    offset_row = offsets[0]
    feat_cols = scale_ls.shape[0]

    zh = lax.axis_index("zh")
    own_blocks = lax.all_gather(stream_rows, "y", axis=0, tiled=False)
    partner_blocks = lax.all_gather(swap_pair(stream_rows), "y", axis=0, tiled=False)
    live_rows = jnp.where(
        zh == 0,
        jnp.stack([own_blocks, partner_blocks], axis=1),
        jnp.stack([partner_blocks, own_blocks], axis=1),
    ).reshape(-1, stream_rows.shape[1])[:LIVE_ROWS]
    normed = layer_norm(live_rows, ln_gain, ln_bias)

    projected = jnp.concatenate(
        [
            jnp.dot(normed, w_q, preferred_element_type=jnp.float32),
            jnp.dot(normed, w_k, preferred_element_type=jnp.float32),
            jnp.dot(normed, w_v, preferred_element_type=jnp.float32),
        ],
        axis=1,
    )
    segment, coord_one, coord_two = row_layout(side_row, offset_row, LIVE_ROWS)
    cosine, sine_tab = rotary_tables(coord_one, coord_two, HEAD)
    queries = rotate(
        projected[:, :head_cols].reshape(LIVE_ROWS, local_heads, HEAD), cosine, sine_tab
    ).astype(jnp.bfloat16)
    key_rows = rotate(
        projected[:, head_cols : 2 * head_cols].reshape(LIVE_ROWS, local_heads, HEAD),
        cosine,
        sine_tab,
    ).astype(jnp.bfloat16)
    value_rows = (
        projected[:, 2 * head_cols :].astype(jnp.bfloat16).reshape(LIVE_ROWS, local_heads, HEAD)
    )
    attended = attention(queries, key_rows, value_rows, segment).reshape(LIVE_ROWS, head_cols)

    source_rows, valid = merge_rows(side_row[0], offset_row[0])
    padded_rows = jnp.concatenate(
        [source_rows, jnp.zeros((MERGE_PAD - source_rows.shape[0],), jnp.int32)]
    )
    merged_attended = jnp.dot(
        one_hot(padded_rows, LIVE_ROWS), attended, preferred_element_type=jnp.float32
    ).astype(jnp.bfloat16)
    partial_sum = jnp.dot(merged_attended, w_o, preferred_element_type=jnp.float32).astype(
        jnp.bfloat16
    )
    group_count = 1
    for name in DP_AXES:
        group_count *= lax.axis_size(name)
    distance = owners[0, 0] % group_count

    feat_index = lax.axis_index("y") * lax.axis_size("zh") + zh
    residual = jnp.dot(
        one_hot(source_rows, LIVE_ROWS),
        lax.dynamic_slice_in_dim(live_rows, feat_index * feat_cols, feat_cols, axis=1),
        preferred_element_type=jnp.float32,
    )

    quarter = lax.psum_scatter(partial_sum, "y", scatter_dimension=1, tiled=True)
    split = quarter.reshape(MERGE_PAD, 2, feat_cols)[: source_rows.shape[0]]
    mine = jnp.where(zh == 0, split[:, 0], split[:, 1])
    theirs = jnp.where(zh == 0, split[:, 1], split[:, 0])
    branch = mine.astype(jnp.float32) + swap_pair(theirs).astype(jnp.float32)
    updated = (residual + scale_ls * branch).astype(jnp.bfloat16)
    merged = jnp.where(jnp.repeat(valid, 4)[:, None], updated, jnp.zeros_like(updated))
    delivered = shift_by_exchange(merged, distance, group_count).reshape(
        1, CAP, 4, feat_cols
    )
    return delivered[None]


def solution(mesh):
    dp_size, fsdp_size = mesh.devices.shape
    split_mesh = Mesh(
        np.asarray(mesh.devices).reshape(4, dp_size // 8, 2, fsdp_size // 2, 2),
        DP_AXES + FSDP_AXES,
    )
    rows = DP_AXES + FSDP_AXES
    return jax.shard_map(
        body,
        mesh=split_mesh,
        in_specs=(
            P(rows, None),
            P(),
            P(),
            P(None, FSDP_AXES),
            P(None, FSDP_AXES),
            P(None, FSDP_AXES),
            P(FSDP_AXES, None),
            P(FSDP_AXES),
            P(DP_AXES, None),
            P(DP_AXES, None),
            P(),
        ),
        out_specs=P(DP_AXES, None, None, None, FSDP_AXES),
        check_vma=False,
    )
```

```python
import math

import jax
import jax.numpy as jnp
import numpy as np
from jax import lax
from jax.sharding import Mesh
from jax.sharding import PartitionSpec as P

HEAD = 128
EXTRA = 5
CAP = 81
LIVE_ROWS = 336
MERGE_PAD = 328

norm_eps = 1e-06

DP_AXES = ("x", "zl", "c")
FSDP_AXES = ("y", "zh")


def layer_norm(raw_rows, ln_gain, ln_bias):
    values = raw_rows.astype(jnp.float32)
    centre = jnp.mean(values, axis=-1, keepdims=True)
    spread = jnp.mean(jnp.square(values - centre), axis=-1, keepdims=True)
    return ((values - centre) * lax.rsqrt(spread + norm_eps) * ln_gain + ln_bias).astype(
        jnp.bfloat16
    )


def row_layout(side_row, offset_row, count):
    row_ids = jnp.arange(count, dtype=jnp.int32)
    lengths = EXTRA + side_row * side_row
    inside = (
        (row_ids[:, None] >= offset_row[None, :])
        & (row_ids[:, None] < (offset_row + lengths)[None, :])
    ).astype(jnp.int32)
    covered = jnp.sum(inside, axis=1)
    image_ids = jnp.arange(side_row.shape[0], dtype=jnp.int32)
    segment = jnp.sum(inside * image_ids[None, :], axis=1) + (1 - covered) * side_row.shape[0]
    first_row = jnp.sum(inside * offset_row[None, :], axis=1)
    side_len = jnp.sum(inside * side_row[None, :], axis=1) + (1 - covered)
    patch_id = row_ids - first_row - EXTRA
    is_patch = (covered == 1) & (patch_id >= 0)
    clipped = jnp.maximum(patch_id, 0)
    across = clipped // side_len
    along = clipped % side_len
    side_float = side_len.astype(jnp.float32)
    coord_one = jnp.where(
        is_patch,
        (2 * across + 1).astype(jnp.float32) / side_float - 1.0,
        jnp.zeros_like(side_float),
    )
    coord_two = jnp.where(
        is_patch, (2 * along + 1).astype(jnp.float32) / side_float - 1.0, jnp.zeros_like(side_float)
    )
    return (segment, coord_one, coord_two)


def rotary_tables(coord_one, coord_two, head_size):
    dims = jnp.arange(head_size, dtype=jnp.int32)
    first_half = dims < head_size // 2
    freq_index = (dims % (head_size // 4)).astype(jnp.float32)
    rates = 3.0 * jnp.power(jnp.ones_like(freq_index) * 1.2, freq_index)
    coords = jnp.where(first_half[None, :], coord_one[:, None], coord_two[:, None])
    angles = coords * rates[None, :]
    return (jnp.cos(angles), jnp.sin(angles))


def rotate(tensor, cosine, sine_tab):
    row_count, head_count, head_size = tensor.shape
    quarters = tensor.reshape(row_count, head_count, 2, 2, head_size // 4)
    turned = jnp.stack([-quarters[:, :, :, 1], quarters[:, :, :, 0]], axis=3).reshape(tensor.shape)
    return tensor * cosine[:, None, :] + turned * sine_tab[:, None, :]


def softmax_rounded(scores):
    top = jnp.max(scores, axis=-1, keepdims=True)
    expo = jnp.exp(scores - top)
    return (expo / jnp.sum(expo, axis=-1, keepdims=True)).astype(jnp.bfloat16)


def merge_rows(side_len, offset):
    slot = jnp.arange(CAP, dtype=jnp.int32)
    half_side = side_len // 2
    across = slot // half_side
    along = slot % half_side
    valid = slot < half_side * half_side
    corner = jnp.arange(4, dtype=jnp.int32)
    source_rows = (
        offset
        + EXTRA
        + (2 * across[:, None] + corner[None, :] // 2) * side_len
        + 2 * along[:, None]
        + corner[None, :] % 2
    )
    source_rows = jnp.where(valid[:, None], source_rows, jnp.zeros_like(source_rows))
    return source_rows.reshape(CAP * 4), valid


def attention(queries, key_rows, value_rows, segment):
    scores = jnp.einsum(
        "qhd,khd->hqk", queries, key_rows, preferred_element_type=jnp.float32
    ) / math.sqrt(HEAD)
    allowed = segment[None, :, None] == segment[None, None, :]
    scores = jnp.where(allowed, scores, jnp.full_like(scores, -1e30))
    weights = softmax_rounded(scores)
    return jnp.einsum(
        "hqk,khd->qhd", weights, value_rows, preferred_element_type=jnp.float32
    ).astype(jnp.bfloat16)


def one_hot(rows, count):
    return (rows[:, None] == jnp.arange(count, dtype=jnp.int32)[None, :]).astype(jnp.bfloat16)


def swap_pair(array):
    return lax.ppermute(array, "zh", [(0, 1), (1, 0)])


def shift_dp(block, distance):
    count = 1
    for name in DP_AXES:
        count *= lax.axis_size(name)

    def branch(by):
        if by == 0:
            return lambda v: v
        pairs = [(i, (i + by) % count) for i in range(count)]
        return lambda v: lax.ppermute(v, DP_AXES, pairs)

    return lax.switch(distance, [branch(by) for by in range(count)], block)


def shift_by_exchange(payload, distance, count):
    size = payload.size
    lanes = 128
    rows = -(-size // (count * lanes))
    rows = -(-rows // 16) * 16
    flat = jnp.pad(payload.reshape(-1), (0, count * rows * lanes - size))
    pieces = lax.all_to_all(flat.reshape(count, rows, lanes), DP_AXES, 0, 0, tiled=True)
    rolled = jnp.roll(pieces, distance, axis=0)
    back = lax.all_to_all(rolled, DP_AXES, 0, 0, tiled=True)
    return back.reshape(-1)[:size].reshape(payload.shape)


def deliver_halves(mine, theirs, distance):
    count = 1
    for name in DP_AXES:
        count *= lax.axis_size(name)

    def branch(by):
        if by == 0:
            return lambda a, b: (a, swap_pair(b))
        same = [(i, (i + by) % count) for i in range(count)]
        across = [
            (2 * i + h, 2 * ((i + by) % count) + 1 - h) for i in range(count) for h in range(2)
        ]
        return lambda a, b: (
            lax.ppermute(a, DP_AXES, same),
            lax.ppermute(b, DP_AXES + ("zh",), across),
        )

    return lax.switch(distance, [branch(by) for by in range(count)], mine, theirs)


def body(stream_rows, ln_gain, ln_bias, w_q, w_k, w_v, w_o, scale_ls, sides, offsets, owners):
    head_cols = w_q.shape[1]
    local_heads = head_cols // HEAD
    side_row = sides[0]
    offset_row = offsets[0]
    feat_cols = scale_ls.shape[0]

    zh = lax.axis_index("zh")
    y_index = lax.axis_index("y")
    y_count = lax.axis_size("y")
    own_blocks = lax.all_gather(stream_rows, "y", axis=0, tiled=False)
    partner = swap_pair(stream_rows)
    live_blocks = -(-LIVE_ROWS // (2 * stream_rows.shape[0]))
    candidates = [partner] + [
        lax.ppermute(
            partner, "y", [(src, (src + by) % y_count) for src in range(live_blocks)]
        )
        for by in range(1, y_count)
    ]
    slots = (y_index - jnp.arange(live_blocks, dtype=jnp.int32)) % y_count
    partner_blocks = jnp.take(jnp.stack(candidates), slots, axis=0)
    own_blocks = own_blocks[:live_blocks]
    live_rows = jnp.where(
        zh == 0,
        jnp.stack([own_blocks, partner_blocks], axis=1),
        jnp.stack([partner_blocks, own_blocks], axis=1),
    ).reshape(-1, stream_rows.shape[1])[:LIVE_ROWS]
    normed = layer_norm(live_rows, ln_gain, ln_bias)

    projected = jnp.concatenate(
        [
            jnp.dot(normed, w_q, preferred_element_type=jnp.float32),
            jnp.dot(normed, w_k, preferred_element_type=jnp.float32),
            jnp.dot(normed, w_v, preferred_element_type=jnp.float32),
        ],
        axis=1,
    )
    segment, coord_one, coord_two = row_layout(side_row, offset_row, LIVE_ROWS)
    cosine, sine_tab = rotary_tables(coord_one, coord_two, HEAD)
    queries = rotate(
        projected[:, :head_cols].reshape(LIVE_ROWS, local_heads, HEAD), cosine, sine_tab
    ).astype(jnp.bfloat16)
    key_rows = rotate(
        projected[:, head_cols : 2 * head_cols].reshape(LIVE_ROWS, local_heads, HEAD),
        cosine,
        sine_tab,
    ).astype(jnp.bfloat16)
    value_rows = (
        projected[:, 2 * head_cols :].astype(jnp.bfloat16).reshape(LIVE_ROWS, local_heads, HEAD)
    )
    attended = attention(queries, key_rows, value_rows, segment).reshape(LIVE_ROWS, head_cols)

    source_rows, valid = merge_rows(side_row[0], offset_row[0])
    padded_rows = jnp.concatenate(
        [source_rows, jnp.zeros((MERGE_PAD - source_rows.shape[0],), jnp.int32)]
    )
    merged_attended = jnp.dot(
        one_hot(padded_rows, LIVE_ROWS), attended, preferred_element_type=jnp.float32
    ).astype(jnp.bfloat16)
    partial_sum = jnp.dot(merged_attended, w_o, preferred_element_type=jnp.float32).astype(
        jnp.bfloat16
    )
    group_count = 1
    for name in DP_AXES:
        group_count *= lax.axis_size(name)
    distance = owners[0, 0] % group_count

    feat_index = lax.axis_index("y") * lax.axis_size("zh") + zh
    residual = jnp.dot(
        one_hot(source_rows, LIVE_ROWS),
        lax.dynamic_slice_in_dim(live_rows, feat_index * feat_cols, feat_cols, axis=1),
        preferred_element_type=jnp.float32,
    )

    quarter = lax.psum_scatter(partial_sum, "y", scatter_dimension=1, tiled=True)
    split = quarter.reshape(MERGE_PAD, 2, feat_cols)[: source_rows.shape[0]]
    mine = jnp.where(zh == 0, split[:, 0], split[:, 1])
    theirs = jnp.where(zh == 0, split[:, 1], split[:, 0])
    branch = mine.astype(jnp.float32) + swap_pair(theirs).astype(jnp.float32)
    updated = (residual + scale_ls * branch).astype(jnp.bfloat16)
    merged = jnp.where(jnp.repeat(valid, 4)[:, None], updated, jnp.zeros_like(updated))
    delivered = shift_by_exchange(merged, distance, group_count).reshape(
        1, CAP, 4, feat_cols
    )
    return delivered[None]


def solution(mesh):
    dp_size, fsdp_size = mesh.devices.shape
    split_mesh = Mesh(
        np.asarray(mesh.devices).reshape(4, dp_size // 8, 2, fsdp_size // 2, 2),
        DP_AXES + FSDP_AXES,
    )
    rows = DP_AXES + FSDP_AXES
    return jax.shard_map(
        body,
        mesh=split_mesh,
        in_specs=(
            P(rows, None),
            P(),
            P(),
            P(None, FSDP_AXES),
            P(None, FSDP_AXES),
            P(None, FSDP_AXES),
            P(FSDP_AXES, None),
            P(FSDP_AXES),
            P(DP_AXES, None),
            P(DP_AXES, None),
            P(),
        ),
        out_specs=P(DP_AXES, None, None, None, FSDP_AXES),
        check_vma=False,
    )
```

```python
import math

import jax
import jax.numpy as jnp
import numpy as np
from jax import lax
from jax.sharding import Mesh
from jax.sharding import PartitionSpec as P

HEAD = 128
EXTRA = 5
CAP = 81
LIVE_ROWS = 336
MERGE_PAD = 328

norm_eps = 1e-06

DP_AXES = ("x", "zl", "c")
FSDP_AXES = ("y", "zh")


def layer_norm(raw_rows, ln_gain, ln_bias):
    values = raw_rows.astype(jnp.float32)
    centre = jnp.mean(values, axis=-1, keepdims=True)
    spread = jnp.mean(jnp.square(values - centre), axis=-1, keepdims=True)
    return ((values - centre) * lax.rsqrt(spread + norm_eps) * ln_gain + ln_bias).astype(
        jnp.bfloat16
    )


def row_layout(side_row, offset_row, row_ids):
    lengths = EXTRA + side_row * side_row
    inside = (
        (row_ids[:, None] >= offset_row[None, :])
        & (row_ids[:, None] < (offset_row + lengths)[None, :])
    ).astype(jnp.int32)
    covered = jnp.sum(inside, axis=1)
    image_ids = jnp.arange(side_row.shape[0], dtype=jnp.int32)
    segment = jnp.sum(inside * image_ids[None, :], axis=1) + (1 - covered) * side_row.shape[0]
    first_row = jnp.sum(inside * offset_row[None, :], axis=1)
    side_len = jnp.sum(inside * side_row[None, :], axis=1) + (1 - covered)
    patch_id = row_ids - first_row - EXTRA
    is_patch = (covered == 1) & (patch_id >= 0)
    clipped = jnp.maximum(patch_id, 0)
    across = clipped // side_len
    along = clipped % side_len
    side_float = side_len.astype(jnp.float32)
    coord_one = jnp.where(
        is_patch,
        (2 * across + 1).astype(jnp.float32) / side_float - 1.0,
        jnp.zeros_like(side_float),
    )
    coord_two = jnp.where(
        is_patch, (2 * along + 1).astype(jnp.float32) / side_float - 1.0, jnp.zeros_like(side_float)
    )
    return (segment, coord_one, coord_two)


def rotary_tables(coord_one, coord_two, head_size):
    dims = jnp.arange(head_size, dtype=jnp.int32)
    first_half = dims < head_size // 2
    freq_index = (dims % (head_size // 4)).astype(jnp.float32)
    rates = 3.0 * jnp.power(jnp.ones_like(freq_index) * 1.2, freq_index)
    coords = jnp.where(first_half[None, :], coord_one[:, None], coord_two[:, None])
    angles = coords * rates[None, :]
    return (jnp.cos(angles), jnp.sin(angles))


def rotate(tensor, cosine, sine_tab):
    row_count, head_count, head_size = tensor.shape
    quarters = tensor.reshape(row_count, head_count, 2, 2, head_size // 4)
    turned = jnp.stack([-quarters[:, :, :, 1], quarters[:, :, :, 0]], axis=3).reshape(tensor.shape)
    return tensor * cosine[:, None, :] + turned * sine_tab[:, None, :]


def softmax_rounded(scores):
    top = jnp.max(scores, axis=-1, keepdims=True)
    expo = jnp.exp(scores - top)
    return (expo / jnp.sum(expo, axis=-1, keepdims=True)).astype(jnp.bfloat16)


def merge_rows(side_len, offset):
    slot = jnp.arange(CAP, dtype=jnp.int32)
    half_side = side_len // 2
    across = slot // half_side
    along = slot % half_side
    valid = slot < half_side * half_side
    corner = jnp.arange(4, dtype=jnp.int32)
    source_rows = (
        offset
        + EXTRA
        + (2 * across[:, None] + corner[None, :] // 2) * side_len
        + 2 * along[:, None]
        + corner[None, :] % 2
    )
    source_rows = jnp.where(valid[:, None], source_rows, jnp.zeros_like(source_rows))
    return source_rows.reshape(CAP * 4), valid


def attention(queries, key_rows, value_rows, segment):
    scores = jnp.einsum(
        "qhd,khd->hqk", queries, key_rows, preferred_element_type=jnp.float32
    ) / math.sqrt(HEAD)
    allowed = segment[None, :, None] == segment[None, None, :]
    scores = jnp.where(allowed, scores, jnp.full_like(scores, -1e30))
    weights = softmax_rounded(scores)
    return jnp.einsum(
        "hqk,khd->qhd", weights, value_rows, preferred_element_type=jnp.float32
    ).astype(jnp.bfloat16)


def position_of(rows, row_ids):
    hits = rows[:, None] == row_ids[None, :]
    return jnp.argmax(hits, axis=1).astype(jnp.int32)


def one_hot(rows, count):
    return (rows[:, None] == jnp.arange(count, dtype=jnp.int32)[None, :]).astype(jnp.bfloat16)


def swap_pair(array):
    return lax.ppermute(array, "zh", [(0, 1), (1, 0)])


def shift_dp(block, distance):
    count = 1
    for name in DP_AXES:
        count *= lax.axis_size(name)

    def branch(by):
        if by == 0:
            return lambda v: v
        pairs = [(i, (i + by) % count) for i in range(count)]
        return lambda v: lax.ppermute(v, DP_AXES, pairs)

    return lax.switch(distance, [branch(by) for by in range(count)], block)


def shift_by_exchange(payload, distance, count):
    size = payload.size
    lanes = 128
    rows = -(-size // (count * lanes))
    rows = -(-rows // 16) * 16
    flat = jnp.pad(payload.reshape(-1), (0, count * rows * lanes - size))
    pieces = lax.all_to_all(flat.reshape(count, rows, lanes), DP_AXES, 0, 0, tiled=True)
    rolled = jnp.roll(pieces, distance, axis=0)
    back = lax.all_to_all(rolled, DP_AXES, 0, 0, tiled=True)
    return back.reshape(-1)[:size].reshape(payload.shape)


def deliver_halves(mine, theirs, distance):
    count = 1
    for name in DP_AXES:
        count *= lax.axis_size(name)

    def branch(by):
        if by == 0:
            return lambda a, b: (a, swap_pair(b))
        same = [(i, (i + by) % count) for i in range(count)]
        across = [
            (2 * i + h, 2 * ((i + by) % count) + 1 - h) for i in range(count) for h in range(2)
        ]
        return lambda a, b: (
            lax.ppermute(a, DP_AXES, same),
            lax.ppermute(b, DP_AXES + ("zh",), across),
        )

    return lax.switch(distance, [branch(by) for by in range(count)], mine, theirs)


def body(stream_rows, ln_gain, ln_bias, w_q, w_k, w_v, w_o, scale_ls, sides, offsets, owners):
    head_cols = w_q.shape[1]
    local_heads = head_cols // HEAD
    side_row = sides[0]
    offset_row = offsets[0]
    feat_cols = scale_ls.shape[0]

    zh = lax.axis_index("zh")
    y_index = lax.axis_index("y")
    y_count = lax.axis_size("y")
    own_blocks = lax.all_gather(stream_rows, "y", axis=0, tiled=False)
    partner = swap_pair(stream_rows)
    live_blocks = -(-LIVE_ROWS // (2 * stream_rows.shape[0]))
    candidates = [partner] + [
        lax.ppermute(
            partner, "y", [(src, (src + by) % y_count) for src in range(live_blocks)]
        )
        for by in range(1, y_count)
    ]
    block = stream_rows.shape[0]
    in_block = jnp.arange(block, dtype=jnp.int32)
    own_ids = (2 * jnp.arange(live_blocks, dtype=jnp.int32)[:, None] + zh) * block + in_block
    from_y = (y_index - jnp.arange(y_count, dtype=jnp.int32)) % y_count
    partner_ids = (2 * from_y[:, None] + 1 - zh) * block + in_block
    row_ids = jnp.concatenate([own_ids.reshape(-1), partner_ids.reshape(-1)])
    live_rows = jnp.concatenate(
        [own_blocks[:live_blocks].reshape(-1, stream_rows.shape[1])] + candidates, axis=0
    )
    row_count = row_ids.shape[0]
    normed = layer_norm(live_rows, ln_gain, ln_bias)

    projected = jnp.concatenate(
        [
            jnp.dot(normed, w_q, preferred_element_type=jnp.float32),
            jnp.dot(normed, w_k, preferred_element_type=jnp.float32),
            jnp.dot(normed, w_v, preferred_element_type=jnp.float32),
        ],
        axis=1,
    )
    segment, coord_one, coord_two = row_layout(side_row, offset_row, row_ids)
    cosine, sine_tab = rotary_tables(coord_one, coord_two, HEAD)
    queries = rotate(
        projected[:, :head_cols].reshape(row_count, local_heads, HEAD), cosine, sine_tab
    ).astype(jnp.bfloat16)
    key_rows = rotate(
        projected[:, head_cols : 2 * head_cols].reshape(row_count, local_heads, HEAD),
        cosine,
        sine_tab,
    ).astype(jnp.bfloat16)
    value_rows = (
        projected[:, 2 * head_cols :].astype(jnp.bfloat16).reshape(row_count, local_heads, HEAD)
    )
    attended = attention(queries, key_rows, value_rows, segment).reshape(row_count, head_cols)

    source_rows, valid = merge_rows(side_row[0], offset_row[0])
    padded_rows = jnp.concatenate(
        [source_rows, jnp.zeros((MERGE_PAD - source_rows.shape[0],), jnp.int32)]
    )
    merged_attended = jnp.dot(
        one_hot(position_of(padded_rows, row_ids), row_count), attended, preferred_element_type=jnp.float32
    ).astype(jnp.bfloat16)
    partial_sum = jnp.dot(merged_attended, w_o, preferred_element_type=jnp.float32).astype(
        jnp.bfloat16
    )
    group_count = 1
    for name in DP_AXES:
        group_count *= lax.axis_size(name)
    distance = owners[0, 0] % group_count

    feat_index = lax.axis_index("y") * lax.axis_size("zh") + zh
    residual = jnp.dot(
        one_hot(position_of(source_rows, row_ids), row_count),
        lax.dynamic_slice_in_dim(live_rows, feat_index * feat_cols, feat_cols, axis=1),
        preferred_element_type=jnp.float32,
    )

    quarter = lax.psum_scatter(partial_sum, "y", scatter_dimension=1, tiled=True)
    split = quarter.reshape(MERGE_PAD, 2, feat_cols)[: source_rows.shape[0]]
    mine = jnp.where(zh == 0, split[:, 0], split[:, 1])
    theirs = jnp.where(zh == 0, split[:, 1], split[:, 0])
    branch = mine.astype(jnp.float32) + swap_pair(theirs).astype(jnp.float32)
    updated = (residual + scale_ls * branch).astype(jnp.bfloat16)
    merged = jnp.where(jnp.repeat(valid, 4)[:, None], updated, jnp.zeros_like(updated))
    delivered = shift_by_exchange(merged, distance, group_count).reshape(
        1, CAP, 4, feat_cols
    )
    return delivered[None]


def solution(mesh):
    dp_size, fsdp_size = mesh.devices.shape
    split_mesh = Mesh(
        np.asarray(mesh.devices).reshape(4, dp_size // 8, 2, fsdp_size // 2, 2),
        DP_AXES + FSDP_AXES,
    )
    rows = DP_AXES + FSDP_AXES
    return jax.shard_map(
        body,
        mesh=split_mesh,
        in_specs=(
            P(rows, None),
            P(),
            P(),
            P(None, FSDP_AXES),
            P(None, FSDP_AXES),
            P(None, FSDP_AXES),
            P(FSDP_AXES, None),
            P(FSDP_AXES),
            P(DP_AXES, None),
            P(DP_AXES, None),
            P(),
        ),
        out_specs=P(DP_AXES, None, None, None, FSDP_AXES),
        check_vma=False,
    )
```

```python
import math

import jax
import jax.numpy as jnp
import numpy as np
from jax import lax
from jax.sharding import Mesh
from jax.sharding import PartitionSpec as P

HEAD = 128
EXTRA = 5
CAP = 81
LIVE_ROWS = 336
MERGE_PAD = 328

norm_eps = 1e-06

DP_AXES = ("x", "zl", "c")
FSDP_AXES = ("y", "zh")


def layer_norm(raw_rows, ln_gain, ln_bias):
    values = raw_rows.astype(jnp.float32)
    centre = jnp.mean(values, axis=-1, keepdims=True)
    spread = jnp.mean(jnp.square(values - centre), axis=-1, keepdims=True)
    return ((values - centre) * lax.rsqrt(spread + norm_eps) * ln_gain + ln_bias).astype(
        jnp.bfloat16
    )


def row_layout(side_row, offset_row, row_ids):
    lengths = EXTRA + side_row * side_row
    inside = (
        (row_ids[:, None] >= offset_row[None, :])
        & (row_ids[:, None] < (offset_row + lengths)[None, :])
    ).astype(jnp.int32)
    covered = jnp.sum(inside, axis=1)
    image_ids = jnp.arange(side_row.shape[0], dtype=jnp.int32)
    segment = jnp.sum(inside * image_ids[None, :], axis=1) + (1 - covered) * side_row.shape[0]
    first_row = jnp.sum(inside * offset_row[None, :], axis=1)
    side_len = jnp.sum(inside * side_row[None, :], axis=1) + (1 - covered)
    patch_id = row_ids - first_row - EXTRA
    is_patch = (covered == 1) & (patch_id >= 0)
    clipped = jnp.maximum(patch_id, 0)
    across = clipped // side_len
    along = clipped % side_len
    side_float = side_len.astype(jnp.float32)
    coord_one = jnp.where(
        is_patch,
        (2 * across + 1).astype(jnp.float32) / side_float - 1.0,
        jnp.zeros_like(side_float),
    )
    coord_two = jnp.where(
        is_patch, (2 * along + 1).astype(jnp.float32) / side_float - 1.0, jnp.zeros_like(side_float)
    )
    return (segment, coord_one, coord_two)


def rotary_tables(coord_one, coord_two, head_size):
    dims = jnp.arange(head_size, dtype=jnp.int32)
    first_half = dims < head_size // 2
    freq_index = (dims % (head_size // 4)).astype(jnp.float32)
    rates = 3.0 * jnp.power(jnp.ones_like(freq_index) * 1.2, freq_index)
    coords = jnp.where(first_half[None, :], coord_one[:, None], coord_two[:, None])
    angles = coords * rates[None, :]
    return (jnp.cos(angles), jnp.sin(angles))


def rotate(tensor, cosine, sine_tab):
    row_count, head_count, head_size = tensor.shape
    quarters = tensor.reshape(row_count, head_count, 2, 2, head_size // 4)
    turned = jnp.stack([-quarters[:, :, :, 1], quarters[:, :, :, 0]], axis=3).reshape(tensor.shape)
    return tensor * cosine[:, None, :] + turned * sine_tab[:, None, :]


def softmax_rounded(scores):
    top = jnp.max(scores, axis=-1, keepdims=True)
    expo = jnp.exp(scores - top)
    return (expo / jnp.sum(expo, axis=-1, keepdims=True)).astype(jnp.bfloat16)


def merge_rows(side_len, offset):
    slot = jnp.arange(CAP, dtype=jnp.int32)
    half_side = side_len // 2
    across = slot // half_side
    along = slot % half_side
    valid = slot < half_side * half_side
    corner = jnp.arange(4, dtype=jnp.int32)
    source_rows = (
        offset
        + EXTRA
        + (2 * across[:, None] + corner[None, :] // 2) * side_len
        + 2 * along[:, None]
        + corner[None, :] % 2
    )
    source_rows = jnp.where(valid[:, None], source_rows, jnp.zeros_like(source_rows))
    return source_rows.reshape(CAP * 4), valid


def attention(queries, key_rows, value_rows, segment):
    scores = jnp.einsum(
        "qhd,khd->hqk", queries, key_rows, preferred_element_type=jnp.float32
    ) / math.sqrt(HEAD)
    allowed = segment[None, :, None] == segment[None, None, :]
    scores = jnp.where(allowed, scores, jnp.full_like(scores, -1e30))
    weights = softmax_rounded(scores)
    return jnp.einsum(
        "hqk,khd->qhd", weights, value_rows, preferred_element_type=jnp.float32
    ).astype(jnp.bfloat16)


def position_of(rows, row_ids):
    hits = rows[:, None] == row_ids[None, :]
    return jnp.argmax(hits, axis=1).astype(jnp.int32)


def one_hot(rows, count):
    return (rows[:, None] == jnp.arange(count, dtype=jnp.int32)[None, :]).astype(jnp.bfloat16)


def swap_pair(array):
    return lax.ppermute(array, "zh", [(0, 1), (1, 0)])


def shift_dp(block, distance):
    count = 1
    for name in DP_AXES:
        count *= lax.axis_size(name)

    def branch(by):
        if by == 0:
            return lambda v: v
        pairs = [(i, (i + by) % count) for i in range(count)]
        return lambda v: lax.ppermute(v, DP_AXES, pairs)

    return lax.switch(distance, [branch(by) for by in range(count)], block)


def shift_by_exchange(payload, distance, count):
    size = payload.size
    lanes = 128
    rows = -(-size // (count * lanes))
    rows = -(-rows // 16) * 16
    flat = jnp.pad(payload.reshape(-1), (0, count * rows * lanes - size))
    pieces = lax.all_to_all(flat.reshape(count, rows, lanes), DP_AXES, 0, 0, tiled=True)
    rolled = jnp.roll(pieces, distance, axis=0)
    back = lax.all_to_all(rolled, DP_AXES, 0, 0, tiled=True)
    return back.reshape(-1)[:size].reshape(payload.shape)


def deliver_halves(mine, theirs, distance):
    count = 1
    for name in DP_AXES:
        count *= lax.axis_size(name)

    def branch(by):
        if by == 0:
            return lambda a, b: (a, swap_pair(b))
        same = [(i, (i + by) % count) for i in range(count)]
        across = [
            (2 * i + h, 2 * ((i + by) % count) + 1 - h) for i in range(count) for h in range(2)
        ]
        return lambda a, b: (
            lax.ppermute(a, DP_AXES, same),
            lax.ppermute(b, DP_AXES + ("zh",), across),
        )

    return lax.switch(distance, [branch(by) for by in range(count)], mine, theirs)


def body(stream_rows, ln_gain, ln_bias, w_q, w_k, w_v, w_o, scale_ls, sides, offsets, owners):
    head_cols = w_q.shape[1]
    local_heads = head_cols // HEAD
    side_row = sides[0]
    offset_row = offsets[0]
    feat_cols = scale_ls.shape[0]

    zh = lax.axis_index("zh")
    y_index = lax.axis_index("y")
    y_count = lax.axis_size("y")
    own_blocks = lax.all_gather(stream_rows, "y", axis=0, tiled=False)
    partner = swap_pair(stream_rows)
    live_blocks = -(-LIVE_ROWS // (2 * stream_rows.shape[0]))
    candidates = [partner] + [
        lax.ppermute(
            partner, "y", [(src, (src + by) % y_count) for src in range(live_blocks)]
        )
        for by in range(1, y_count)
    ]
    block = stream_rows.shape[0]
    in_block = jnp.arange(block, dtype=jnp.int32)
    own_ids = (2 * jnp.arange(live_blocks, dtype=jnp.int32)[:, None] + zh) * block + in_block
    from_y = (y_index - jnp.arange(y_count, dtype=jnp.int32)) % y_count
    partner_ids = (2 * from_y[:, None] + 1 - zh) * block + in_block
    row_ids = jnp.concatenate([own_ids.reshape(-1), partner_ids.reshape(-1)])
    live_rows = jnp.concatenate(
        [own_blocks[:live_blocks].reshape(-1, stream_rows.shape[1])] + candidates, axis=0
    )
    row_count = row_ids.shape[0]
    normed = layer_norm(live_rows, ln_gain, ln_bias)

    projected = jnp.concatenate(
        [
            jnp.dot(normed, w_q, preferred_element_type=jnp.float32),
            jnp.dot(normed, w_k, preferred_element_type=jnp.float32),
            jnp.dot(normed, w_v, preferred_element_type=jnp.float32),
        ],
        axis=1,
    )
    segment, coord_one, coord_two = row_layout(side_row, offset_row, row_ids)
    cosine, sine_tab = rotary_tables(coord_one, coord_two, HEAD)
    queries = rotate(
        projected[:, :head_cols].reshape(row_count, local_heads, HEAD), cosine, sine_tab
    ).astype(jnp.bfloat16)
    key_rows = rotate(
        projected[:, head_cols : 2 * head_cols].reshape(row_count, local_heads, HEAD),
        cosine,
        sine_tab,
    ).astype(jnp.bfloat16)
    value_rows = (
        projected[:, 2 * head_cols :].astype(jnp.bfloat16).reshape(row_count, local_heads, HEAD)
    )
    attended = attention(queries, key_rows, value_rows, segment).reshape(row_count, head_cols)

    source_rows, valid = merge_rows(side_row[0], offset_row[0])
    padded_rows = jnp.concatenate(
        [source_rows, jnp.zeros((MERGE_PAD - source_rows.shape[0],), jnp.int32)]
    )
    merged_attended = jnp.dot(
        one_hot(position_of(padded_rows, row_ids), row_count), attended, preferred_element_type=jnp.float32
    ).astype(jnp.bfloat16)
    partial_sum = jnp.dot(merged_attended, w_o, preferred_element_type=jnp.float32).astype(
        jnp.bfloat16
    )
    group_count = 1
    for name in DP_AXES:
        group_count *= lax.axis_size(name)
    distance = owners[0, 0] % group_count

    feat_index = lax.axis_index("y") * lax.axis_size("zh") + zh
    residual = jnp.dot(
        one_hot(position_of(source_rows, row_ids), row_count),
        lax.dynamic_slice_in_dim(live_rows, feat_index * feat_cols, feat_cols, axis=1),
        preferred_element_type=jnp.float32,
    )

    quarter_cols = feat_cols * lax.axis_size("zh")
    on_sc = MERGE_PAD // 2
    quarter_sc = lax.psum_scatter(partial_sum[:on_sc], "y", scatter_dimension=1, tiled=True)
    rest = partial_sum[on_sc:]
    quarter_pp = lax.dynamic_slice_in_dim(rest, y_index * quarter_cols, quarter_cols, axis=1)
    quarter_pp = quarter_pp.astype(jnp.float32)
    for by in range(1, y_count):
        chunk = lax.dynamic_slice_in_dim(
            rest, ((y_index + by) % y_count) * quarter_cols, quarter_cols, axis=1
        )
        moved = lax.ppermute(chunk, "y", [(src, (src + by) % y_count) for src in range(y_count)])
        quarter_pp = quarter_pp + moved.astype(jnp.float32)
    quarter = jnp.concatenate([quarter_sc, quarter_pp.astype(jnp.bfloat16)], axis=0)
    split = quarter.reshape(MERGE_PAD, 2, feat_cols)[: source_rows.shape[0]]
    mine = jnp.where(zh == 0, split[:, 0], split[:, 1])
    theirs = jnp.where(zh == 0, split[:, 1], split[:, 0])
    branch = mine.astype(jnp.float32) + swap_pair(theirs).astype(jnp.float32)
    updated = (residual + scale_ls * branch).astype(jnp.bfloat16)
    merged = jnp.where(jnp.repeat(valid, 4)[:, None], updated, jnp.zeros_like(updated))
    delivered = shift_by_exchange(merged, distance, group_count).reshape(
        1, CAP, 4, feat_cols
    )
    return delivered[None]


def solution(mesh):
    dp_size, fsdp_size = mesh.devices.shape
    split_mesh = Mesh(
        np.asarray(mesh.devices).reshape(4, dp_size // 8, 2, fsdp_size // 2, 2),
        DP_AXES + FSDP_AXES,
    )
    rows = DP_AXES + FSDP_AXES
    return jax.shard_map(
        body,
        mesh=split_mesh,
        in_specs=(
            P(rows, None),
            P(),
            P(),
            P(None, FSDP_AXES),
            P(None, FSDP_AXES),
            P(None, FSDP_AXES),
            P(FSDP_AXES, None),
            P(FSDP_AXES),
            P(DP_AXES, None),
            P(DP_AXES, None),
            P(),
        ),
        out_specs=P(DP_AXES, None, None, None, FSDP_AXES),
        check_vma=False,
    )
```

```python
import math

import jax
import jax.numpy as jnp
import numpy as np
from jax import lax
from jax.sharding import Mesh
from jax.sharding import PartitionSpec as P

HEAD = 128
EXTRA = 5
CAP = 81
LIVE_ROWS = 336
MERGE_PAD = 328

norm_eps = 1e-06

DP_AXES = ("x", "zl", "c")
FSDP_AXES = ("y", "zh")


def layer_norm(raw_rows, ln_gain, ln_bias):
    values = raw_rows.astype(jnp.float32)
    centre = jnp.mean(values, axis=-1, keepdims=True)
    spread = jnp.mean(jnp.square(values - centre), axis=-1, keepdims=True)
    return ((values - centre) * lax.rsqrt(spread + norm_eps) * ln_gain + ln_bias).astype(
        jnp.bfloat16
    )


def row_layout(side_row, offset_row, row_ids):
    lengths = EXTRA + side_row * side_row
    inside = (
        (row_ids[:, None] >= offset_row[None, :])
        & (row_ids[:, None] < (offset_row + lengths)[None, :])
    ).astype(jnp.int32)
    covered = jnp.sum(inside, axis=1)
    image_ids = jnp.arange(side_row.shape[0], dtype=jnp.int32)
    segment = jnp.sum(inside * image_ids[None, :], axis=1) + (1 - covered) * side_row.shape[0]
    first_row = jnp.sum(inside * offset_row[None, :], axis=1)
    side_len = jnp.sum(inside * side_row[None, :], axis=1) + (1 - covered)
    patch_id = row_ids - first_row - EXTRA
    is_patch = (covered == 1) & (patch_id >= 0)
    clipped = jnp.maximum(patch_id, 0)
    across = clipped // side_len
    along = clipped % side_len
    side_float = side_len.astype(jnp.float32)
    coord_one = jnp.where(
        is_patch,
        (2 * across + 1).astype(jnp.float32) / side_float - 1.0,
        jnp.zeros_like(side_float),
    )
    coord_two = jnp.where(
        is_patch, (2 * along + 1).astype(jnp.float32) / side_float - 1.0, jnp.zeros_like(side_float)
    )
    return (segment, coord_one, coord_two)


def rotary_tables(coord_one, coord_two, head_size):
    dims = jnp.arange(head_size, dtype=jnp.int32)
    first_half = dims < head_size // 2
    freq_index = (dims % (head_size // 4)).astype(jnp.float32)
    rates = 3.0 * jnp.power(jnp.ones_like(freq_index) * 1.2, freq_index)
    coords = jnp.where(first_half[None, :], coord_one[:, None], coord_two[:, None])
    angles = coords * rates[None, :]
    return (jnp.cos(angles), jnp.sin(angles))


def rotate(tensor, cosine, sine_tab):
    row_count, head_count, head_size = tensor.shape
    quarters = tensor.reshape(row_count, head_count, 2, 2, head_size // 4)
    turned = jnp.stack([-quarters[:, :, :, 1], quarters[:, :, :, 0]], axis=3).reshape(tensor.shape)
    return tensor * cosine[:, None, :] + turned * sine_tab[:, None, :]


def softmax_rounded(scores):
    top = jnp.max(scores, axis=-1, keepdims=True)
    expo = jnp.exp(scores - top)
    return (expo / jnp.sum(expo, axis=-1, keepdims=True)).astype(jnp.bfloat16)


def merge_rows(side_len, offset):
    slot = jnp.arange(CAP, dtype=jnp.int32)
    half_side = side_len // 2
    across = slot // half_side
    along = slot % half_side
    valid = slot < half_side * half_side
    corner = jnp.arange(4, dtype=jnp.int32)
    source_rows = (
        offset
        + EXTRA
        + (2 * across[:, None] + corner[None, :] // 2) * side_len
        + 2 * along[:, None]
        + corner[None, :] % 2
    )
    source_rows = jnp.where(valid[:, None], source_rows, jnp.zeros_like(source_rows))
    return source_rows.reshape(CAP * 4), valid


def attention(queries, key_rows, value_rows, segment):
    scores = jnp.einsum(
        "qhd,khd->hqk", queries, key_rows, preferred_element_type=jnp.float32
    ) / math.sqrt(HEAD)
    allowed = segment[None, :, None] == segment[None, None, :]
    scores = jnp.where(allowed, scores, jnp.full_like(scores, -1e30))
    weights = softmax_rounded(scores)
    return jnp.einsum(
        "hqk,khd->qhd", weights, value_rows, preferred_element_type=jnp.float32
    ).astype(jnp.bfloat16)


def position_of(rows, row_ids):
    hits = rows[:, None] == row_ids[None, :]
    return jnp.argmax(hits, axis=1).astype(jnp.int32)


def one_hot(rows, count):
    return (rows[:, None] == jnp.arange(count, dtype=jnp.int32)[None, :]).astype(jnp.bfloat16)


def swap_pair(array):
    return lax.ppermute(array, "zh", [(0, 1), (1, 0)])


def shift_dp(block, distance):
    count = 1
    for name in DP_AXES:
        count *= lax.axis_size(name)

    def branch(by):
        if by == 0:
            return lambda v: v
        pairs = [(i, (i + by) % count) for i in range(count)]
        return lambda v: lax.ppermute(v, DP_AXES, pairs)

    return lax.switch(distance, [branch(by) for by in range(count)], block)


def shift_by_exchange(payload, distance, count):
    size = payload.size
    lanes = 128
    rows = -(-size // (count * lanes))
    rows = -(-rows // 16) * 16
    flat = jnp.pad(payload.reshape(-1), (0, count * rows * lanes - size))
    pieces = lax.all_to_all(flat.reshape(count, rows, lanes), DP_AXES, 0, 0, tiled=True)
    rolled = jnp.roll(pieces, distance, axis=0)
    back = lax.all_to_all(rolled, DP_AXES, 0, 0, tiled=True)
    return back.reshape(-1)[:size].reshape(payload.shape)


def deliver_halves(mine, theirs, distance):
    count = 1
    for name in DP_AXES:
        count *= lax.axis_size(name)

    def branch(by):
        if by == 0:
            return lambda a, b: (a, swap_pair(b))
        same = [(i, (i + by) % count) for i in range(count)]
        across = [
            (2 * i + h, 2 * ((i + by) % count) + 1 - h) for i in range(count) for h in range(2)
        ]
        return lambda a, b: (
            lax.ppermute(a, DP_AXES, same),
            lax.ppermute(b, DP_AXES + ("zh",), across),
        )

    return lax.switch(distance, [branch(by) for by in range(count)], mine, theirs)


def body(stream_rows, ln_gain, ln_bias, w_q, w_k, w_v, w_o, scale_ls, sides, offsets, owners):
    head_cols = w_q.shape[1]
    local_heads = head_cols // HEAD
    side_row = sides[0]
    offset_row = offsets[0]
    feat_cols = scale_ls.shape[0]

    zh = lax.axis_index("zh")
    y_index = lax.axis_index("y")
    y_count = lax.axis_size("y")
    own_blocks = lax.all_gather(stream_rows, "y", axis=0, tiled=False)
    partner = swap_pair(stream_rows)
    live_blocks = -(-LIVE_ROWS // (2 * stream_rows.shape[0]))
    candidates = [partner] + [
        lax.ppermute(
            partner, "y", [(src, (src + by) % y_count) for src in range(live_blocks)]
        )
        for by in range(1, y_count)
    ]
    block = stream_rows.shape[0]
    in_block = jnp.arange(block, dtype=jnp.int32)
    own_ids = (2 * jnp.arange(live_blocks, dtype=jnp.int32)[:, None] + zh) * block + in_block
    from_y = (y_index - jnp.arange(y_count, dtype=jnp.int32)) % y_count
    partner_ids = (2 * from_y[:, None] + 1 - zh) * block + in_block
    row_ids = jnp.concatenate([own_ids.reshape(-1), partner_ids.reshape(-1)])
    live_rows = jnp.concatenate(
        [own_blocks[:live_blocks].reshape(-1, stream_rows.shape[1])] + candidates, axis=0
    )
    row_count = row_ids.shape[0]
    normed = layer_norm(live_rows, ln_gain, ln_bias)

    projected = jnp.concatenate(
        [
            jnp.dot(normed, w_q, preferred_element_type=jnp.float32),
            jnp.dot(normed, w_k, preferred_element_type=jnp.float32),
            jnp.dot(normed, w_v, preferred_element_type=jnp.float32),
        ],
        axis=1,
    )
    segment, coord_one, coord_two = row_layout(side_row, offset_row, row_ids)
    cosine, sine_tab = rotary_tables(coord_one, coord_two, HEAD)
    queries = rotate(
        projected[:, :head_cols].reshape(row_count, local_heads, HEAD), cosine, sine_tab
    ).astype(jnp.bfloat16)
    key_rows = rotate(
        projected[:, head_cols : 2 * head_cols].reshape(row_count, local_heads, HEAD),
        cosine,
        sine_tab,
    ).astype(jnp.bfloat16)
    value_rows = (
        projected[:, 2 * head_cols :].astype(jnp.bfloat16).reshape(row_count, local_heads, HEAD)
    )
    attended = attention(queries, key_rows, value_rows, segment).reshape(row_count, head_cols)

    source_rows, valid = merge_rows(side_row[0], offset_row[0])
    padded_rows = jnp.concatenate(
        [source_rows, jnp.zeros((MERGE_PAD - source_rows.shape[0],), jnp.int32)]
    )
    merged_attended = jnp.dot(
        one_hot(position_of(padded_rows, row_ids), row_count), attended, preferred_element_type=jnp.float32
    ).astype(jnp.bfloat16)
    partial_sum = jnp.dot(merged_attended, w_o, preferred_element_type=jnp.float32).astype(
        jnp.bfloat16
    )
    group_count = 1
    for name in DP_AXES:
        group_count *= lax.axis_size(name)
    distance = owners[0, 0] % group_count

    feat_index = lax.axis_index("y") * lax.axis_size("zh") + zh
    residual = jnp.dot(
        one_hot(position_of(source_rows, row_ids), row_count),
        lax.dynamic_slice_in_dim(live_rows, feat_index * feat_cols, feat_cols, axis=1),
        preferred_element_type=jnp.float32,
    )

    quarter_cols = feat_cols * lax.axis_size("zh")
    quarter = lax.dynamic_slice_in_dim(
        partial_sum, y_index * quarter_cols, quarter_cols, axis=1
    ).astype(jnp.float32)
    for by in range(1, y_count):
        chunk = lax.dynamic_slice_in_dim(
            partial_sum, ((y_index + by) % y_count) * quarter_cols, quarter_cols, axis=1
        )
        moved = lax.ppermute(chunk, "y", [(src, (src + by) % y_count) for src in range(y_count)])
        quarter = quarter + moved.astype(jnp.float32)
    quarter = quarter.astype(jnp.bfloat16)
    split = quarter.reshape(MERGE_PAD, 2, feat_cols)[: source_rows.shape[0]]
    mine = jnp.where(zh == 0, split[:, 0], split[:, 1])
    theirs = jnp.where(zh == 0, split[:, 1], split[:, 0])
    branch = mine.astype(jnp.float32) + swap_pair(theirs).astype(jnp.float32)
    updated = (residual + scale_ls * branch).astype(jnp.bfloat16)
    merged = jnp.where(jnp.repeat(valid, 4)[:, None], updated, jnp.zeros_like(updated))
    delivered = shift_by_exchange(merged, distance, group_count).reshape(
        1, CAP, 4, feat_cols
    )
    return delivered[None]


def solution(mesh):
    dp_size, fsdp_size = mesh.devices.shape
    split_mesh = Mesh(
        np.asarray(mesh.devices).reshape(4, dp_size // 8, 2, fsdp_size // 2, 2),
        DP_AXES + FSDP_AXES,
    )
    rows = DP_AXES + FSDP_AXES
    return jax.shard_map(
        body,
        mesh=split_mesh,
        in_specs=(
            P(rows, None),
            P(),
            P(),
            P(None, FSDP_AXES),
            P(None, FSDP_AXES),
            P(None, FSDP_AXES),
            P(FSDP_AXES, None),
            P(FSDP_AXES),
            P(DP_AXES, None),
            P(DP_AXES, None),
            P(),
        ),
        out_specs=P(DP_AXES, None, None, None, FSDP_AXES),
        check_vma=False,
    )
```

```python
import math

import jax
import jax.numpy as jnp
import numpy as np
from jax import lax
from jax.sharding import Mesh
from jax.sharding import PartitionSpec as P

HEAD = 128
EXTRA = 5
CAP = 81
LIVE_ROWS = 336
MERGE_PAD = 328

norm_eps = 1e-06

DP_AXES = ("x", "zl", "c")
FSDP_AXES = ("y", "zh")


def layer_norm(raw_rows, ln_gain, ln_bias):
    values = raw_rows.astype(jnp.float32)
    centre = jnp.mean(values, axis=-1, keepdims=True)
    spread = jnp.mean(jnp.square(values - centre), axis=-1, keepdims=True)
    return ((values - centre) * lax.rsqrt(spread + norm_eps) * ln_gain + ln_bias).astype(
        jnp.bfloat16
    )


def row_layout(side_row, offset_row, row_ids):
    lengths = EXTRA + side_row * side_row
    inside = (
        (row_ids[:, None] >= offset_row[None, :])
        & (row_ids[:, None] < (offset_row + lengths)[None, :])
    ).astype(jnp.int32)
    covered = jnp.sum(inside, axis=1)
    image_ids = jnp.arange(side_row.shape[0], dtype=jnp.int32)
    segment = jnp.sum(inside * image_ids[None, :], axis=1) + (1 - covered) * side_row.shape[0]
    first_row = jnp.sum(inside * offset_row[None, :], axis=1)
    side_len = jnp.sum(inside * side_row[None, :], axis=1) + (1 - covered)
    patch_id = row_ids - first_row - EXTRA
    is_patch = (covered == 1) & (patch_id >= 0)
    clipped = jnp.maximum(patch_id, 0)
    across = clipped // side_len
    along = clipped % side_len
    side_float = side_len.astype(jnp.float32)
    coord_one = jnp.where(
        is_patch,
        (2 * across + 1).astype(jnp.float32) / side_float - 1.0,
        jnp.zeros_like(side_float),
    )
    coord_two = jnp.where(
        is_patch, (2 * along + 1).astype(jnp.float32) / side_float - 1.0, jnp.zeros_like(side_float)
    )
    return (segment, coord_one, coord_two)


def rotary_tables(coord_one, coord_two, head_size):
    dims = jnp.arange(head_size, dtype=jnp.int32)
    first_half = dims < head_size // 2
    freq_index = (dims % (head_size // 4)).astype(jnp.float32)
    rates = 3.0 * jnp.power(jnp.ones_like(freq_index) * 1.2, freq_index)
    coords = jnp.where(first_half[None, :], coord_one[:, None], coord_two[:, None])
    angles = coords * rates[None, :]
    return (jnp.cos(angles), jnp.sin(angles))


def rotate(tensor, cosine, sine_tab):
    row_count, head_count, head_size = tensor.shape
    quarters = tensor.reshape(row_count, head_count, 2, 2, head_size // 4)
    turned = jnp.stack([-quarters[:, :, :, 1], quarters[:, :, :, 0]], axis=3).reshape(tensor.shape)
    return tensor * cosine[:, None, :] + turned * sine_tab[:, None, :]


def softmax_rounded(scores):
    top = jnp.max(scores, axis=-1, keepdims=True)
    expo = jnp.exp(scores - top)
    return (expo / jnp.sum(expo, axis=-1, keepdims=True)).astype(jnp.bfloat16)


def merge_rows(side_len, offset):
    slot = jnp.arange(CAP, dtype=jnp.int32)
    half_side = side_len // 2
    across = slot // half_side
    along = slot % half_side
    valid = slot < half_side * half_side
    corner = jnp.arange(4, dtype=jnp.int32)
    source_rows = (
        offset
        + EXTRA
        + (2 * across[:, None] + corner[None, :] // 2) * side_len
        + 2 * along[:, None]
        + corner[None, :] % 2
    )
    source_rows = jnp.where(valid[:, None], source_rows, jnp.zeros_like(source_rows))
    return source_rows.reshape(CAP * 4), valid


def attention(queries, key_rows, value_rows, segment):
    scores = jnp.einsum(
        "qhd,khd->hqk", queries, key_rows, preferred_element_type=jnp.float32
    ) / math.sqrt(HEAD)
    allowed = segment[None, :, None] == segment[None, None, :]
    scores = jnp.where(allowed, scores, jnp.full_like(scores, -1e30))
    weights = softmax_rounded(scores)
    return jnp.einsum(
        "hqk,khd->qhd", weights, value_rows, preferred_element_type=jnp.float32
    ).astype(jnp.bfloat16)


def position_of(rows, row_ids):
    hits = rows[:, None] == row_ids[None, :]
    return jnp.argmax(hits, axis=1).astype(jnp.int32)


def one_hot(rows, count):
    return (rows[:, None] == jnp.arange(count, dtype=jnp.int32)[None, :]).astype(jnp.bfloat16)


def swap_pair(array):
    return lax.ppermute(array, "zh", [(0, 1), (1, 0)])


def shift_dp(block, distance):
    count = 1
    for name in DP_AXES:
        count *= lax.axis_size(name)

    def branch(by):
        if by == 0:
            return lambda v: v
        pairs = [(i, (i + by) % count) for i in range(count)]
        return lambda v: lax.ppermute(v, DP_AXES, pairs)

    return lax.switch(distance, [branch(by) for by in range(count)], block)


def scatter_pieces(payload):
    count = lax.axis_size(DP_AXES)
    size = payload.size
    lanes = 128
    rows = -(-size // (count * lanes))
    rows = -(-rows // 16) * 16
    flat = jnp.pad(payload.reshape(-1), (0, count * rows * lanes - size))
    return lax.all_to_all(flat.reshape(count, rows, lanes), DP_AXES, 0, 0, tiled=True)


def gather_pieces(pieces, distance, shape):
    size = math.prod(shape)
    back = lax.all_to_all(jnp.roll(pieces, distance, axis=0), DP_AXES, 0, 0, tiled=True)
    return back.reshape(-1)[:size].reshape(shape)


def shift_by_exchange(payload, distance, count):
    size = payload.size
    lanes = 128
    rows = -(-size // (count * lanes))
    rows = -(-rows // 16) * 16
    flat = jnp.pad(payload.reshape(-1), (0, count * rows * lanes - size))
    pieces = lax.all_to_all(flat.reshape(count, rows, lanes), DP_AXES, 0, 0, tiled=True)
    rolled = jnp.roll(pieces, distance, axis=0)
    back = lax.all_to_all(rolled, DP_AXES, 0, 0, tiled=True)
    return back.reshape(-1)[:size].reshape(payload.shape)


def deliver_halves(mine, theirs, distance):
    count = 1
    for name in DP_AXES:
        count *= lax.axis_size(name)

    def branch(by):
        if by == 0:
            return lambda a, b: (a, swap_pair(b))
        same = [(i, (i + by) % count) for i in range(count)]
        across = [
            (2 * i + h, 2 * ((i + by) % count) + 1 - h) for i in range(count) for h in range(2)
        ]
        return lambda a, b: (
            lax.ppermute(a, DP_AXES, same),
            lax.ppermute(b, DP_AXES + ("zh",), across),
        )

    return lax.switch(distance, [branch(by) for by in range(count)], mine, theirs)


def body(stream_rows, ln_gain, ln_bias, w_q, w_k, w_v, w_o, scale_ls, sides, offsets, owners):
    head_cols = w_q.shape[1]
    local_heads = head_cols // HEAD
    side_row = sides[0]
    offset_row = offsets[0]
    feat_cols = scale_ls.shape[0]

    zh = lax.axis_index("zh")
    y_index = lax.axis_index("y")
    y_count = lax.axis_size("y")
    own_blocks = lax.all_gather(stream_rows, "y", axis=0, tiled=False)
    partner = swap_pair(stream_rows)
    live_blocks = -(-LIVE_ROWS // (2 * stream_rows.shape[0]))
    candidates = [partner] + [
        lax.ppermute(
            partner, "y", [(src, (src + by) % y_count) for src in range(live_blocks)]
        )
        for by in range(1, y_count)
    ]
    block = stream_rows.shape[0]
    in_block = jnp.arange(block, dtype=jnp.int32)
    own_ids = (2 * jnp.arange(live_blocks, dtype=jnp.int32)[:, None] + zh) * block + in_block
    from_y = (y_index - jnp.arange(y_count, dtype=jnp.int32)) % y_count
    partner_ids = (2 * from_y[:, None] + 1 - zh) * block + in_block
    row_ids = jnp.concatenate([own_ids.reshape(-1), partner_ids.reshape(-1)])
    live_rows = jnp.concatenate(
        [own_blocks[:live_blocks].reshape(-1, stream_rows.shape[1])] + candidates, axis=0
    )
    row_count = row_ids.shape[0]
    normed = layer_norm(live_rows, ln_gain, ln_bias)

    projected = jnp.concatenate(
        [
            jnp.dot(normed, w_q, preferred_element_type=jnp.float32),
            jnp.dot(normed, w_k, preferred_element_type=jnp.float32),
            jnp.dot(normed, w_v, preferred_element_type=jnp.float32),
        ],
        axis=1,
    )
    segment, coord_one, coord_two = row_layout(side_row, offset_row, row_ids)
    cosine, sine_tab = rotary_tables(coord_one, coord_two, HEAD)
    queries = rotate(
        projected[:, :head_cols].reshape(row_count, local_heads, HEAD), cosine, sine_tab
    ).astype(jnp.bfloat16)
    key_rows = rotate(
        projected[:, head_cols : 2 * head_cols].reshape(row_count, local_heads, HEAD),
        cosine,
        sine_tab,
    ).astype(jnp.bfloat16)
    value_rows = (
        projected[:, 2 * head_cols :].astype(jnp.bfloat16).reshape(row_count, local_heads, HEAD)
    )
    attended = attention(queries, key_rows, value_rows, segment).reshape(row_count, head_cols)

    source_rows, valid = merge_rows(side_row[0], offset_row[0])
    padded_rows = jnp.concatenate(
        [source_rows, jnp.zeros((MERGE_PAD - source_rows.shape[0],), jnp.int32)]
    )
    merged_attended = jnp.dot(
        one_hot(position_of(padded_rows, row_ids), row_count), attended, preferred_element_type=jnp.float32
    ).astype(jnp.bfloat16)
    partial_sum = jnp.dot(merged_attended, w_o, preferred_element_type=jnp.float32).astype(
        jnp.bfloat16
    )
    group_count = 1
    for name in DP_AXES:
        group_count *= lax.axis_size(name)
    distance = owners[0, 0] % group_count

    feat_index = lax.axis_index("y") * lax.axis_size("zh") + zh
    keep = jnp.repeat(valid, 4)[:, None]
    residual = jnp.dot(
        one_hot(position_of(source_rows, row_ids), row_count),
        lax.dynamic_slice_in_dim(live_rows, feat_index * feat_cols, feat_cols, axis=1),
        preferred_element_type=jnp.float32,
    ).astype(jnp.bfloat16)
    residual_pieces = scatter_pieces(jnp.where(keep, residual, jnp.zeros_like(residual)))

    quarter_cols = feat_cols * lax.axis_size("zh")
    quarter = lax.dynamic_slice_in_dim(
        partial_sum, y_index * quarter_cols, quarter_cols, axis=1
    ).astype(jnp.float32)
    for by in range(1, y_count):
        chunk = lax.dynamic_slice_in_dim(
            partial_sum, ((y_index + by) % y_count) * quarter_cols, quarter_cols, axis=1
        )
        moved = lax.ppermute(chunk, "y", [(src, (src + by) % y_count) for src in range(y_count)])
        quarter = quarter + moved.astype(jnp.float32)
    quarter = quarter.astype(jnp.bfloat16)
    split = quarter.reshape(MERGE_PAD, 2, feat_cols)[: source_rows.shape[0]]
    mine = jnp.where(zh == 0, split[:, 0], split[:, 1])
    theirs = jnp.where(zh == 0, split[:, 1], split[:, 0])
    mine_pieces = scatter_pieces(jnp.where(keep, mine, jnp.zeros_like(mine)))
    theirs = swap_pair(theirs)
    theirs_pieces = scatter_pieces(jnp.where(keep, theirs, jnp.zeros_like(theirs)))
    piece_size = mine_pieces.shape[1] * mine_pieces.shape[2]
    piece_index = lax.axis_index(DP_AXES)
    cols = (piece_index * piece_size + jnp.arange(piece_size, dtype=jnp.int32)) % feat_cols
    piece_scale = jnp.take(scale_ls, cols).reshape(mine_pieces.shape[1:])
    branch = mine_pieces.astype(jnp.float32) + theirs_pieces.astype(jnp.float32)
    updated = (residual_pieces.astype(jnp.float32) + piece_scale * branch).astype(jnp.bfloat16)
    delivered = gather_pieces(updated, distance, residual.shape).reshape(1, CAP, 4, feat_cols)
    return delivered[None]


def solution(mesh):
    dp_size, fsdp_size = mesh.devices.shape
    split_mesh = Mesh(
        np.asarray(mesh.devices).reshape(4, dp_size // 8, 2, fsdp_size // 2, 2),
        DP_AXES + FSDP_AXES,
    )
    rows = DP_AXES + FSDP_AXES
    return jax.shard_map(
        body,
        mesh=split_mesh,
        in_specs=(
            P(rows, None),
            P(),
            P(),
            P(None, FSDP_AXES),
            P(None, FSDP_AXES),
            P(None, FSDP_AXES),
            P(FSDP_AXES, None),
            P(FSDP_AXES),
            P(DP_AXES, None),
            P(DP_AXES, None),
            P(),
        ),
        out_specs=P(DP_AXES, None, None, None, FSDP_AXES),
        check_vma=False,
    )
```

```python
import math

import jax
import jax.numpy as jnp
import numpy as np
from jax import lax
from jax.sharding import Mesh
from jax.sharding import PartitionSpec as P

HEAD = 128
EXTRA = 5
CAP = 81
LIVE_ROWS = 336
MERGE_PAD = 328

norm_eps = 1e-06

DP_AXES = ("x", "zl", "c")
FSDP_AXES = ("y", "zh")


def layer_norm(raw_rows, ln_gain, ln_bias):
    values = raw_rows.astype(jnp.float32)
    centre = jnp.mean(values, axis=-1, keepdims=True)
    spread = jnp.mean(jnp.square(values - centre), axis=-1, keepdims=True)
    return ((values - centre) * lax.rsqrt(spread + norm_eps) * ln_gain + ln_bias).astype(
        jnp.bfloat16
    )


def row_layout(side_row, offset_row, row_ids):
    lengths = EXTRA + side_row * side_row
    inside = (
        (row_ids[:, None] >= offset_row[None, :])
        & (row_ids[:, None] < (offset_row + lengths)[None, :])
    ).astype(jnp.int32)
    covered = jnp.sum(inside, axis=1)
    image_ids = jnp.arange(side_row.shape[0], dtype=jnp.int32)
    segment = jnp.sum(inside * image_ids[None, :], axis=1) + (1 - covered) * side_row.shape[0]
    first_row = jnp.sum(inside * offset_row[None, :], axis=1)
    side_len = jnp.sum(inside * side_row[None, :], axis=1) + (1 - covered)
    patch_id = row_ids - first_row - EXTRA
    is_patch = (covered == 1) & (patch_id >= 0)
    clipped = jnp.maximum(patch_id, 0)
    across = clipped // side_len
    along = clipped % side_len
    side_float = side_len.astype(jnp.float32)
    coord_one = jnp.where(
        is_patch,
        (2 * across + 1).astype(jnp.float32) / side_float - 1.0,
        jnp.zeros_like(side_float),
    )
    coord_two = jnp.where(
        is_patch, (2 * along + 1).astype(jnp.float32) / side_float - 1.0, jnp.zeros_like(side_float)
    )
    return (segment, coord_one, coord_two)


def rotary_tables(coord_one, coord_two, head_size):
    dims = jnp.arange(head_size, dtype=jnp.int32)
    first_half = dims < head_size // 2
    freq_index = (dims % (head_size // 4)).astype(jnp.float32)
    rates = 3.0 * jnp.power(jnp.ones_like(freq_index) * 1.2, freq_index)
    coords = jnp.where(first_half[None, :], coord_one[:, None], coord_two[:, None])
    angles = coords * rates[None, :]
    return (jnp.cos(angles), jnp.sin(angles))


def rotate(tensor, cosine, sine_tab):
    row_count, head_count, head_size = tensor.shape
    quarters = tensor.reshape(row_count, head_count, 2, 2, head_size // 4)
    turned = jnp.stack([-quarters[:, :, :, 1], quarters[:, :, :, 0]], axis=3).reshape(tensor.shape)
    return tensor * cosine[:, None, :] + turned * sine_tab[:, None, :]


def softmax_rounded(scores):
    top = jnp.max(scores, axis=-1, keepdims=True)
    expo = jnp.exp(scores - top)
    return (expo / jnp.sum(expo, axis=-1, keepdims=True)).astype(jnp.bfloat16)


def merge_rows(side_len, offset):
    slot = jnp.arange(CAP, dtype=jnp.int32)
    half_side = side_len // 2
    across = slot // half_side
    along = slot % half_side
    valid = slot < half_side * half_side
    corner = jnp.arange(4, dtype=jnp.int32)
    source_rows = (
        offset
        + EXTRA
        + (2 * across[:, None] + corner[None, :] // 2) * side_len
        + 2 * along[:, None]
        + corner[None, :] % 2
    )
    source_rows = jnp.where(valid[:, None], source_rows, jnp.zeros_like(source_rows))
    return source_rows.reshape(CAP * 4), valid


def attention(queries, key_rows, value_rows, segment):
    scores = jnp.einsum(
        "qhd,khd->hqk", queries, key_rows, preferred_element_type=jnp.float32
    ) / math.sqrt(HEAD)
    allowed = segment[None, :, None] == segment[None, None, :]
    scores = jnp.where(allowed, scores, jnp.full_like(scores, -1e30))
    weights = softmax_rounded(scores)
    return jnp.einsum(
        "hqk,khd->qhd", weights, value_rows, preferred_element_type=jnp.float32
    ).astype(jnp.bfloat16)


def position_of(rows, row_ids):
    hits = rows[:, None] == row_ids[None, :]
    return jnp.argmax(hits, axis=1).astype(jnp.int32)


def one_hot(rows, count):
    return (rows[:, None] == jnp.arange(count, dtype=jnp.int32)[None, :]).astype(jnp.bfloat16)


def swap_pair(array):
    return lax.ppermute(array, "zh", [(0, 1), (1, 0)])


def shift_dp(block, distance):
    count = 1
    for name in DP_AXES:
        count *= lax.axis_size(name)

    def branch(by):
        if by == 0:
            return lambda v: v
        pairs = [(i, (i + by) % count) for i in range(count)]
        return lambda v: lax.ppermute(v, DP_AXES, pairs)

    return lax.switch(distance, [branch(by) for by in range(count)], block)


def shift_by_exchange(payload, distance, count):
    size = payload.size
    lanes = 128
    rows = -(-size // (count * lanes))
    rows = -(-rows // 16) * 16
    flat = jnp.pad(payload.reshape(-1), (0, count * rows * lanes - size))
    pieces = lax.all_to_all(flat.reshape(count, rows, lanes), DP_AXES, 0, 0, tiled=True)
    rolled = jnp.roll(pieces, distance, axis=0)
    back = lax.all_to_all(rolled, DP_AXES, 0, 0, tiled=True)
    return back.reshape(-1)[:size].reshape(payload.shape)


def deliver_halves(mine, theirs, distance):
    count = 1
    for name in DP_AXES:
        count *= lax.axis_size(name)

    def branch(by):
        if by == 0:
            return lambda a, b: (a, swap_pair(b))
        same = [(i, (i + by) % count) for i in range(count)]
        across = [
            (2 * i + h, 2 * ((i + by) % count) + 1 - h) for i in range(count) for h in range(2)
        ]
        return lambda a, b: (
            lax.ppermute(a, DP_AXES, same),
            lax.ppermute(b, DP_AXES + ("zh",), across),
        )

    return lax.switch(distance, [branch(by) for by in range(count)], mine, theirs)


def body(stream_rows, ln_gain, ln_bias, w_q, w_k, w_v, w_o, scale_ls, sides, offsets, owners):
    head_cols = w_q.shape[1]
    local_heads = head_cols // HEAD
    side_row = sides[0]
    offset_row = offsets[0]
    feat_cols = scale_ls.shape[0]

    zh = lax.axis_index("zh")
    y_index = lax.axis_index("y")
    y_count = lax.axis_size("y")
    partner = swap_pair(stream_rows)
    live_blocks = -(-LIVE_ROWS // (2 * stream_rows.shape[0]))

    def spread(rows_in):
        return [rows_in] + [
            lax.ppermute(
                rows_in, "y", [(src, (src + by) % y_count) for src in range(live_blocks)]
            )
            for by in range(1, y_count)
        ]

    own_candidates = spread(stream_rows)
    candidates = spread(partner)
    block = stream_rows.shape[0]
    in_block = jnp.arange(block, dtype=jnp.int32)
    from_y = (y_index - jnp.arange(y_count, dtype=jnp.int32)) % y_count
    own_ids = (2 * from_y[:, None] + zh) * block + in_block
    partner_ids = (2 * from_y[:, None] + 1 - zh) * block + in_block
    row_ids = jnp.concatenate([own_ids.reshape(-1), partner_ids.reshape(-1)])
    live_rows = jnp.concatenate(own_candidates + candidates, axis=0)
    row_count = row_ids.shape[0]
    normed = layer_norm(live_rows, ln_gain, ln_bias)

    projected = jnp.concatenate(
        [
            jnp.dot(normed, w_q, preferred_element_type=jnp.float32),
            jnp.dot(normed, w_k, preferred_element_type=jnp.float32),
            jnp.dot(normed, w_v, preferred_element_type=jnp.float32),
        ],
        axis=1,
    )
    segment, coord_one, coord_two = row_layout(side_row, offset_row, row_ids)
    cosine, sine_tab = rotary_tables(coord_one, coord_two, HEAD)
    queries = rotate(
        projected[:, :head_cols].reshape(row_count, local_heads, HEAD), cosine, sine_tab
    ).astype(jnp.bfloat16)
    key_rows = rotate(
        projected[:, head_cols : 2 * head_cols].reshape(row_count, local_heads, HEAD),
        cosine,
        sine_tab,
    ).astype(jnp.bfloat16)
    value_rows = (
        projected[:, 2 * head_cols :].astype(jnp.bfloat16).reshape(row_count, local_heads, HEAD)
    )
    attended = attention(queries, key_rows, value_rows, segment).reshape(row_count, head_cols)

    source_rows, valid = merge_rows(side_row[0], offset_row[0])
    padded_rows = jnp.concatenate(
        [source_rows, jnp.zeros((MERGE_PAD - source_rows.shape[0],), jnp.int32)]
    )
    merged_attended = jnp.dot(
        one_hot(position_of(padded_rows, row_ids), row_count), attended, preferred_element_type=jnp.float32
    ).astype(jnp.bfloat16)
    partial_sum = jnp.dot(merged_attended, w_o, preferred_element_type=jnp.float32).astype(
        jnp.bfloat16
    )
    group_count = 1
    for name in DP_AXES:
        group_count *= lax.axis_size(name)
    distance = owners[0, 0] % group_count

    feat_index = lax.axis_index("y") * lax.axis_size("zh") + zh
    residual = jnp.dot(
        one_hot(position_of(source_rows, row_ids), row_count),
        lax.dynamic_slice_in_dim(live_rows, feat_index * feat_cols, feat_cols, axis=1),
        preferred_element_type=jnp.float32,
    )

    quarter_cols = feat_cols * lax.axis_size("zh")
    quarter = lax.dynamic_slice_in_dim(
        partial_sum, y_index * quarter_cols, quarter_cols, axis=1
    ).astype(jnp.float32)
    for by in range(1, y_count):
        chunk = lax.dynamic_slice_in_dim(
            partial_sum, ((y_index + by) % y_count) * quarter_cols, quarter_cols, axis=1
        )
        moved = lax.ppermute(chunk, "y", [(src, (src + by) % y_count) for src in range(y_count)])
        quarter = quarter + moved.astype(jnp.float32)
    quarter = quarter.astype(jnp.bfloat16)
    split = quarter.reshape(MERGE_PAD, 2, feat_cols)[: source_rows.shape[0]]
    mine = jnp.where(zh == 0, split[:, 0], split[:, 1])
    theirs = jnp.where(zh == 0, split[:, 1], split[:, 0])
    branch = mine.astype(jnp.float32) + swap_pair(theirs).astype(jnp.float32)
    updated = (residual + scale_ls * branch).astype(jnp.bfloat16)
    merged = jnp.where(jnp.repeat(valid, 4)[:, None], updated, jnp.zeros_like(updated))
    delivered = shift_by_exchange(merged, distance, group_count).reshape(
        1, CAP, 4, feat_cols
    )
    return delivered[None]


def solution(mesh):
    dp_size, fsdp_size = mesh.devices.shape
    split_mesh = Mesh(
        np.asarray(mesh.devices).reshape(4, dp_size // 8, 2, fsdp_size // 2, 2),
        DP_AXES + FSDP_AXES,
    )
    rows = DP_AXES + FSDP_AXES
    return jax.shard_map(
        body,
        mesh=split_mesh,
        in_specs=(
            P(rows, None),
            P(),
            P(),
            P(None, FSDP_AXES),
            P(None, FSDP_AXES),
            P(None, FSDP_AXES),
            P(FSDP_AXES, None),
            P(FSDP_AXES),
            P(DP_AXES, None),
            P(DP_AXES, None),
            P(),
        ),
        out_specs=P(DP_AXES, None, None, None, FSDP_AXES),
        check_vma=False,
    )
```

```python
import math

import jax
import jax.numpy as jnp
import numpy as np
from jax import lax
from jax.sharding import Mesh
from jax.sharding import PartitionSpec as P

HEAD = 128
EXTRA = 5
CAP = 81
LIVE_ROWS = 336
MERGE_PAD = 324

norm_eps = 1e-06

DP_AXES = ("x", "zl", "c")
FSDP_AXES = ("y", "zh")


def layer_norm(raw_rows, ln_gain, ln_bias):
    values = raw_rows.astype(jnp.float32)
    centre = jnp.mean(values, axis=-1, keepdims=True)
    spread = jnp.mean(jnp.square(values - centre), axis=-1, keepdims=True)
    return ((values - centre) * lax.rsqrt(spread + norm_eps) * ln_gain + ln_bias).astype(
        jnp.bfloat16
    )


def row_layout(side_row, offset_row, row_ids):
    lengths = EXTRA + side_row * side_row
    inside = (
        (row_ids[:, None] >= offset_row[None, :])
        & (row_ids[:, None] < (offset_row + lengths)[None, :])
    ).astype(jnp.int32)
    covered = jnp.sum(inside, axis=1)
    image_ids = jnp.arange(side_row.shape[0], dtype=jnp.int32)
    segment = jnp.sum(inside * image_ids[None, :], axis=1) + (1 - covered) * side_row.shape[0]
    first_row = jnp.sum(inside * offset_row[None, :], axis=1)
    side_len = jnp.sum(inside * side_row[None, :], axis=1) + (1 - covered)
    patch_id = row_ids - first_row - EXTRA
    is_patch = (covered == 1) & (patch_id >= 0)
    clipped = jnp.maximum(patch_id, 0)
    across = clipped // side_len
    along = clipped % side_len
    side_float = side_len.astype(jnp.float32)
    coord_one = jnp.where(
        is_patch,
        (2 * across + 1).astype(jnp.float32) / side_float - 1.0,
        jnp.zeros_like(side_float),
    )
    coord_two = jnp.where(
        is_patch, (2 * along + 1).astype(jnp.float32) / side_float - 1.0, jnp.zeros_like(side_float)
    )
    return (segment, coord_one, coord_two)


def rotary_tables(coord_one, coord_two, head_size):
    dims = jnp.arange(head_size, dtype=jnp.int32)
    first_half = dims < head_size // 2
    freq_index = (dims % (head_size // 4)).astype(jnp.float32)
    rates = 3.0 * jnp.power(jnp.ones_like(freq_index) * 1.2, freq_index)
    coords = jnp.where(first_half[None, :], coord_one[:, None], coord_two[:, None])
    angles = coords * rates[None, :]
    return (jnp.cos(angles), jnp.sin(angles))


def rotate(tensor, cosine, sine_tab):
    row_count, head_count, head_size = tensor.shape
    quarters = tensor.reshape(row_count, head_count, 2, 2, head_size // 4)
    turned = jnp.stack([-quarters[:, :, :, 1], quarters[:, :, :, 0]], axis=3).reshape(tensor.shape)
    return tensor * cosine[:, None, :] + turned * sine_tab[:, None, :]


def softmax_rounded(scores):
    top = jnp.max(scores, axis=-1, keepdims=True)
    expo = jnp.exp(scores - top)
    return (expo / jnp.sum(expo, axis=-1, keepdims=True)).astype(jnp.bfloat16)


def merge_rows(side_len, offset):
    slot = jnp.arange(CAP, dtype=jnp.int32)
    half_side = side_len // 2
    across = slot // half_side
    along = slot % half_side
    valid = slot < half_side * half_side
    corner = jnp.arange(4, dtype=jnp.int32)
    source_rows = (
        offset
        + EXTRA
        + (2 * across[:, None] + corner[None, :] // 2) * side_len
        + 2 * along[:, None]
        + corner[None, :] % 2
    )
    source_rows = jnp.where(valid[:, None], source_rows, jnp.zeros_like(source_rows))
    return source_rows.reshape(CAP * 4), valid


def attention(queries, key_rows, value_rows, segment):
    scores = jnp.einsum(
        "qhd,khd->hqk", queries, key_rows, preferred_element_type=jnp.float32
    ) / math.sqrt(HEAD)
    allowed = segment[None, :, None] == segment[None, None, :]
    scores = jnp.where(allowed, scores, jnp.full_like(scores, -1e30))
    weights = softmax_rounded(scores)
    return jnp.einsum(
        "hqk,khd->qhd", weights, value_rows, preferred_element_type=jnp.float32
    ).astype(jnp.bfloat16)


def position_of(rows, row_ids):
    hits = rows[:, None] == row_ids[None, :]
    return jnp.argmax(hits, axis=1).astype(jnp.int32)


def one_hot(rows, count):
    return (rows[:, None] == jnp.arange(count, dtype=jnp.int32)[None, :]).astype(jnp.bfloat16)


def swap_pair(array):
    return lax.ppermute(array, "zh", [(0, 1), (1, 0)])


def shift_dp(block, distance):
    count = 1
    for name in DP_AXES:
        count *= lax.axis_size(name)

    def branch(by):
        if by == 0:
            return lambda v: v
        pairs = [(i, (i + by) % count) for i in range(count)]
        return lambda v: lax.ppermute(v, DP_AXES, pairs)

    return lax.switch(distance, [branch(by) for by in range(count)], block)


def shift_by_exchange(payload, distance, count):
    size = payload.size
    lanes = 128
    rows = -(-size // (count * lanes))
    rows = -(-rows // 16) * 16
    flat = jnp.pad(payload.reshape(-1), (0, count * rows * lanes - size))
    pieces = lax.all_to_all(flat.reshape(count, rows, lanes), DP_AXES, 0, 0, tiled=True)
    rolled = jnp.roll(pieces, distance, axis=0)
    back = lax.all_to_all(rolled, DP_AXES, 0, 0, tiled=True)
    return back.reshape(-1)[:size].reshape(payload.shape)


def deliver_halves(mine, theirs, distance):
    count = 1
    for name in DP_AXES:
        count *= lax.axis_size(name)

    def branch(by):
        if by == 0:
            return lambda a, b: (a, swap_pair(b))
        same = [(i, (i + by) % count) for i in range(count)]
        across = [
            (2 * i + h, 2 * ((i + by) % count) + 1 - h) for i in range(count) for h in range(2)
        ]
        return lambda a, b: (
            lax.ppermute(a, DP_AXES, same),
            lax.ppermute(b, DP_AXES + ("zh",), across),
        )

    return lax.switch(distance, [branch(by) for by in range(count)], mine, theirs)


def body(stream_rows, ln_gain, ln_bias, w_q, w_k, w_v, w_o, scale_ls, sides, offsets, owners):
    head_cols = w_q.shape[1]
    local_heads = head_cols // HEAD
    side_row = sides[0]
    offset_row = offsets[0]
    feat_cols = scale_ls.shape[0]

    zh = lax.axis_index("zh")
    y_index = lax.axis_index("y")
    y_count = lax.axis_size("y")
    partner = swap_pair(stream_rows)
    live_blocks = -(-LIVE_ROWS // (2 * stream_rows.shape[0]))

    def spread(rows_in):
        return [rows_in] + [
            lax.ppermute(
                rows_in, "y", [(src, (src + by) % y_count) for src in range(live_blocks)]
            )
            for by in range(1, y_count)
        ]

    own_candidates = spread(stream_rows)
    candidates = spread(partner)
    block = stream_rows.shape[0]
    in_block = jnp.arange(block, dtype=jnp.int32)
    from_y = (y_index - jnp.arange(y_count, dtype=jnp.int32)) % y_count
    own_ids = (2 * from_y[:, None] + zh) * block + in_block
    partner_ids = (2 * from_y[:, None] + 1 - zh) * block + in_block
    row_ids = jnp.concatenate([own_ids.reshape(-1), partner_ids.reshape(-1)])
    live_rows = jnp.concatenate(own_candidates + candidates, axis=0)
    row_count = row_ids.shape[0]
    normed = layer_norm(live_rows, ln_gain, ln_bias)

    projected = jnp.concatenate(
        [
            jnp.dot(normed, w_q, preferred_element_type=jnp.float32),
            jnp.dot(normed, w_k, preferred_element_type=jnp.float32),
            jnp.dot(normed, w_v, preferred_element_type=jnp.float32),
        ],
        axis=1,
    )
    segment, coord_one, coord_two = row_layout(side_row, offset_row, row_ids)
    cosine, sine_tab = rotary_tables(coord_one, coord_two, HEAD)
    queries = rotate(
        projected[:, :head_cols].reshape(row_count, local_heads, HEAD), cosine, sine_tab
    ).astype(jnp.bfloat16)
    key_rows = rotate(
        projected[:, head_cols : 2 * head_cols].reshape(row_count, local_heads, HEAD),
        cosine,
        sine_tab,
    ).astype(jnp.bfloat16)
    value_rows = (
        projected[:, 2 * head_cols :].astype(jnp.bfloat16).reshape(row_count, local_heads, HEAD)
    )
    attended = attention(queries, key_rows, value_rows, segment).reshape(row_count, head_cols)

    source_rows, valid = merge_rows(side_row[0], offset_row[0])
    padded_rows = jnp.concatenate(
        [source_rows, jnp.zeros((MERGE_PAD - source_rows.shape[0],), jnp.int32)]
    )
    merged_attended = jnp.dot(
        one_hot(position_of(padded_rows, row_ids), row_count), attended, preferred_element_type=jnp.float32
    ).astype(jnp.bfloat16)
    partial_sum = jnp.dot(merged_attended, w_o, preferred_element_type=jnp.float32).astype(
        jnp.bfloat16
    )
    group_count = 1
    for name in DP_AXES:
        group_count *= lax.axis_size(name)
    distance = owners[0, 0] % group_count

    feat_index = lax.axis_index("y") * lax.axis_size("zh") + zh
    residual = jnp.dot(
        one_hot(position_of(source_rows, row_ids), row_count),
        lax.dynamic_slice_in_dim(live_rows, feat_index * feat_cols, feat_cols, axis=1),
        preferred_element_type=jnp.float32,
    )

    quarter_cols = feat_cols * lax.axis_size("zh")
    quarter = lax.dynamic_slice_in_dim(
        partial_sum, y_index * quarter_cols, quarter_cols, axis=1
    ).astype(jnp.float32)
    for by in range(1, y_count):
        chunk = lax.dynamic_slice_in_dim(
            partial_sum, ((y_index + by) % y_count) * quarter_cols, quarter_cols, axis=1
        )
        moved = lax.ppermute(chunk, "y", [(src, (src + by) % y_count) for src in range(y_count)])
        quarter = quarter + moved.astype(jnp.float32)
    quarter = quarter.astype(jnp.bfloat16)
    split = quarter.reshape(MERGE_PAD, 2, feat_cols)[: source_rows.shape[0]]
    mine = jnp.where(zh == 0, split[:, 0], split[:, 1])
    theirs = jnp.where(zh == 0, split[:, 1], split[:, 0])
    branch = mine.astype(jnp.float32) + swap_pair(theirs).astype(jnp.float32)
    updated = (residual + scale_ls * branch).astype(jnp.bfloat16)
    merged = jnp.where(jnp.repeat(valid, 4)[:, None], updated, jnp.zeros_like(updated))
    delivered = shift_by_exchange(merged, distance, group_count).reshape(
        1, CAP, 4, feat_cols
    )
    return delivered[None]


def solution(mesh):
    dp_size, fsdp_size = mesh.devices.shape
    split_mesh = Mesh(
        np.asarray(mesh.devices).reshape(4, dp_size // 8, 2, fsdp_size // 2, 2),
        DP_AXES + FSDP_AXES,
    )
    rows = DP_AXES + FSDP_AXES
    return jax.shard_map(
        body,
        mesh=split_mesh,
        in_specs=(
            P(rows, None),
            P(),
            P(),
            P(None, FSDP_AXES),
            P(None, FSDP_AXES),
            P(None, FSDP_AXES),
            P(FSDP_AXES, None),
            P(FSDP_AXES),
            P(DP_AXES, None),
            P(DP_AXES, None),
            P(),
        ),
        out_specs=P(DP_AXES, None, None, None, FSDP_AXES),
        check_vma=False,
    )
```
